768 devices in a mesh: ctx: 192 (over y, z_lo, x), dp: 4 (over z_hi, core).
Axes of the slice: x: 4, y: 8, z: 12 (z_hi: 2, z_lo: 6; z = z_hi * 6 + z_lo), core: 2. Of those that a mesh axis runs over, the one named last changes fastest.
Arguments:
- att_query: bfloat16 [98304, 4096], P(('dp', 'ctx')), parts along dimension 0, may hold values from -126 to 126
- att_key: bfloat16 [98304, 4096], P(('dp', 'ctx')), parts along dimension 0, may hold values from -6 to 6
- att_value: bfloat16 [98304, 4096], P(('dp', 'ctx')), parts along dimension 0, may hold values from -6 to 6
Outputs:
- attn_out: bfloat16 [98304, 4096], P(('dp', 'ctx')), parts along dimension 0
- attn_lse: float32 [32, 98304], P(None, ('dp', 'ctx')), parts along dimension 1
The draws below stay inside these ranges and needn't reach their ends.
There are 4 independent parts, one for each index of `dp`. The reference program is written for one: setup_inputs(seed, part) draws one part's arguments, and reference() takes and returns one part's arrays. A program takes and returns all parts, laid end to end along the dimension named above; each array names one. Nothing has to cross between parts.
All inputs are finite; a program needn't handle non-finite values.
Results may differ from the reference program's by a relative error of at most 0.0045.
Values may be sent and summed in bfloat16 or wider, within the bound.
No kernel may reach another device: no remote copies, remote signals or barrier semaphores. Data moves between devices by JAX's collectives and lax.ppermute only.
A program may use at most 32 MiB of HBM per device.

```python
import math
import jax
import jax.numpy as jnp
from jax import lax

HEADS = 32
HEAD_DIM = 128
KV_STEPS = 3
TOK_DEV = 128
SEQ = 24576
N_CTX = 192


def attention_pair(key):
    att_width = HEADS * HEAD_DIM
    key_base = jnp.clip(jax.random.normal(jax.random.fold_in(key, 71), (SEQ, att_width), jnp.float32), -6.0, 6.0)
    query_base = jnp.clip(jax.random.normal(jax.random.fold_in(key, 72), (SEQ, att_width), jnp.float32), -6.0, 6.0)
    return (query_base, key_base)


def draw_att_query(key, part):
    return attention_pair(key)[0].astype(jnp.bfloat16)


def draw_att_key(key, part):
    return attention_pair(key)[1].astype(jnp.bfloat16)


def level_of(stream_key, dims, shards, smallest, largest):
    factor_of = 1.0
    for dim, shards_of in shards:
        heights = jax.random.uniform(jax.random.fold_in(jax.random.fold_in(stream_key, 6), dim), (shards_of,), jnp.float32, smallest / len(shards), largest / len(shards))
        factor_of = factor_of * jnp.repeat(jnp.exp(heights), dims[dim] // shards_of).reshape((-1,) + (1,) * (len(dims) - 1 - dim))
    return factor_of


def centred(rng, dims, width, reach, shards=(), kind=jnp.bfloat16):
    drawn = width * jax.random.normal(rng, dims, jnp.float32)
    if shards:
        drawn = drawn * level_of(rng, dims, shards, -0.22, 0.18)
    return jnp.clip(drawn, -reach, reach).astype(kind)


def setup_inputs(seed: int = 0, part: int = 0) -> dict:
    keys = jax.random.split(jax.random.key(seed), 4)
    part_splits = jax.random.split(jax.random.fold_in(keys[3], part), 4)
    return {
        "att_query": draw_att_query(jax.random.fold_in(jax.random.fold_in(keys[3], part), 71), part),
        "att_key": draw_att_key(jax.random.fold_in(jax.random.fold_in(keys[3], part), 71), part),
        "att_value": centred(part_splits[2], (SEQ, HEADS * HEAD_DIM), 1.0, 6.0, ((0, 192),)),
    }


def attend(query_rows, key_rows, value_rows, key_start, query_start):
    row_count = query_rows.shape[0]
    key_count = key_rows.shape[0]
    head_count = query_rows.shape[1] // HEAD_DIM
    queries = query_rows.astype(jnp.float32).reshape(row_count, head_count, HEAD_DIM)
    key_heads = key_rows.astype(jnp.float32).reshape(key_count, head_count, HEAD_DIM)
    value_heads = value_rows.astype(jnp.float32).reshape(key_count, head_count, HEAD_DIM)
    scores = jnp.einsum('thd,shd->hts', queries, key_heads, precision=lax.Precision.HIGHEST) * (1.0 / math.sqrt(HEAD_DIM))
    key_place = key_start + jnp.arange(key_count, dtype=jnp.int32)
    query_place = query_start + jnp.arange(row_count, dtype=jnp.int32)
    allowed = (key_place[None, :] >= 0) & (key_place[None, :] <= query_place[:, None])
    scores = jnp.where(allowed[None], scores, -jnp.inf)
    row_max = lax.optimization_barrier(jnp.max(scores, axis=2, keepdims=True))
    weights = jnp.exp(scores - row_max)
    denominator = lax.optimization_barrier(jnp.sum(weights, axis=2))
    rounded = lax.optimization_barrier(weights.astype(jnp.bfloat16)).astype(jnp.float32)
    mixed = jnp.einsum('hts,shd->thd', rounded, value_heads, precision=lax.Precision.HIGHEST)
    output = (mixed / jnp.transpose(denominator)[:, :, None]).reshape(row_count, head_count * HEAD_DIM).astype(jnp.bfloat16)
    return (output, row_max[:, :, 0] + jnp.log(denominator))

def reference(att_query, att_key, att_value):
    lead_rows = (KV_STEPS - 1) * TOK_DEV
    att_width = att_key.shape[1]
    key_padded = jnp.concatenate([jnp.zeros((lead_rows, att_width), att_key.dtype), att_key], axis=0)
    value_padded = jnp.concatenate([jnp.zeros((lead_rows, att_width), att_value.dtype), att_value], axis=0)

    def attention_block(block_index):
        query_rows = lax.dynamic_slice_in_dim(att_query, block_index * TOK_DEV, TOK_DEV, 0)
        key_rows = lax.dynamic_slice_in_dim(key_padded, block_index * TOK_DEV, KV_STEPS * TOK_DEV, 0)
        value_rows = lax.dynamic_slice_in_dim(value_padded, block_index * TOK_DEV, KV_STEPS * TOK_DEV, 0)
        return attend(query_rows, key_rows, value_rows, (block_index - (KV_STEPS - 1)) * TOK_DEV, block_index * TOK_DEV)
    mixed, log_total = lax.map(attention_block, jnp.arange(N_CTX, dtype=jnp.int32))
    attn_out = mixed.reshape(SEQ, att_width)
    attn_lse = jnp.moveaxis(log_total, 0, 1).reshape(log_total.shape[1], SEQ)
    return (attn_out, attn_lse)
```

```python
import math

import jax
import jax.numpy as jnp
from jax import lax
from jax.experimental import pallas as pl
from jax.experimental.pallas import tpu as pltpu
from jax.sharding import PartitionSpec as P

HEAD_DIM = 128
KV_STEPS = 3
HEADS_PER_STEP = 8


def from_behind(block, axis, distance):
    devices = range(lax.axis_size(axis))
    route = [(i - distance, i) for i in devices if i - distance in devices]
    return lax.ppermute(block, axis, route)


def attention_kernel(block_ref, q_ref, k0_ref, k1_ref, k2_ref, v0_ref, v1_ref, v2_ref, out_ref, lse_ref):
    block_index = block_ref[0]
    rows = q_ref.shape[0]
    scale = 1.0 / math.sqrt(HEAD_DIM)
    row_id = lax.broadcasted_iota(jnp.int32, (rows, rows), 0)
    col_id = lax.broadcasted_iota(jnp.int32, (rows, rows), 1)
    causal = col_id <= row_id
    diagonal = col_id == row_id
    has_prev = block_index >= 1
    has_prev2 = block_index >= 2
    dims = (((1,), (1,)), ((), ()))
    for h in range(HEADS_PER_STEP):
        cols = slice(h * HEAD_DIM, (h + 1) * HEAD_DIM)
        q = q_ref[:, cols]
        s0 = lax.dot_general(q, k0_ref[:, cols], dims, preferred_element_type=jnp.float32) * scale
        s1 = lax.dot_general(q, k1_ref[:, cols], dims, preferred_element_type=jnp.float32) * scale
        s2 = lax.dot_general(q, k2_ref[:, cols], dims, preferred_element_type=jnp.float32) * scale
        s0 = jnp.where(has_prev2, s0, -jnp.inf)
        s1 = jnp.where(has_prev, s1, -jnp.inf)
        s2 = jnp.where(causal, s2, -jnp.inf)
        m = jnp.maximum(
            jnp.maximum(jnp.max(s0, axis=1, keepdims=True), jnp.max(s1, axis=1, keepdims=True)),
            jnp.max(s2, axis=1, keepdims=True),
        )
        p0 = jnp.exp(s0 - m)
        p1 = jnp.exp(s1 - m)
        p2 = jnp.exp(s2 - m)
        total = (
            jnp.sum(p0, axis=1, keepdims=True)
            + jnp.sum(p1, axis=1, keepdims=True)
            + jnp.sum(p2, axis=1, keepdims=True)
        )
        mixed = (
            jnp.dot(p0.astype(jnp.bfloat16), v0_ref[:, cols], preferred_element_type=jnp.float32)
            + jnp.dot(p1.astype(jnp.bfloat16), v1_ref[:, cols], preferred_element_type=jnp.float32)
            + jnp.dot(p2.astype(jnp.bfloat16), v2_ref[:, cols], preferred_element_type=jnp.float32)
        )
        out_ref[:, cols] = (mixed / total).astype(out_ref.dtype)
        lse_col = m + jnp.log(total)
        lse_ref[h : h + 1, :] = jnp.sum(jnp.where(diagonal, lse_col, 0.0), axis=0, keepdims=True)


def attend(block_index, query_rows, keys, values):
    rows, width = query_rows.shape
    head_count = width // HEAD_DIM
    step_width = HEADS_PER_STEP * HEAD_DIM
    steps = head_count // HEADS_PER_STEP
    block = pl.BlockSpec((rows, step_width), lambda g, b: (0, g))
    return pl.pallas_call(
        attention_kernel,
        grid_spec=pltpu.PrefetchScalarGridSpec(
            num_scalar_prefetch=1,
            grid=(steps,),
            in_specs=[block] * 7,
            out_specs=[block, pl.BlockSpec((HEADS_PER_STEP, rows), lambda g, b: (g, 0))],
        ),
        out_shape=[
            jax.ShapeDtypeStruct((rows, width), jnp.bfloat16),
            jax.ShapeDtypeStruct((head_count, rows), jnp.float32),
        ],
    )(block_index, query_rows, *keys, *values)


def shards(att_query, att_key, att_value):
    fetched = []
    for distance in range(1, KV_STEPS):
        source = fetched[-1] if fetched else (att_key, att_value)
        arrived = from_behind((source[0], source[1]), "ctx", 1)
        fetched.append(arrived)
    keys = [received[0] for received in fetched[::-1]] + [att_key]
    values = [received[1] for received in fetched[::-1]] + [att_value]
    block_index = lax.axis_index("ctx").astype(jnp.int32).reshape(1)
    return attend(block_index, att_query, keys, values)


def solution(mesh):
    return jax.shard_map(
        shards,
        mesh=mesh,
        in_specs=(P(("dp", "ctx"), None), P(("dp", "ctx"), None), P(("dp", "ctx"), None)),
        out_specs=(P(("dp", "ctx"), None), P(None, ("dp", "ctx"))),
        check_vma=False,
    )
```

```python
import math

import jax
import jax.numpy as jnp
from jax import lax
from jax.experimental import pallas as pl
from jax.experimental.pallas import tpu as pltpu
from jax.sharding import PartitionSpec as P

HEAD_DIM = 128
HEADS_PER_STEP = 8
CHUNKS = 2
SCALE = 1.0 / math.sqrt(HEAD_DIM)
NT_DIMS = (((1,), (1,)), ((), ()))


def from_behind(block, axis):
    devices = range(lax.axis_size(axis))
    route = [(i - 1, i) for i in devices if i - 1 in devices]
    return lax.ppermute(block, axis, route)


def from_ahead(block, axis):
    devices = range(lax.axis_size(axis))
    route = [(i + 1, i) for i in devices if i + 1 in devices]
    return lax.ppermute(block, axis, route)


def row_to_column(row, diagonal):
    return jnp.sum(jnp.where(diagonal, row, 0.0), axis=1, keepdims=True)


def column_to_row(column, diagonal):
    return jnp.sum(jnp.where(diagonal, column, 0.0), axis=0, keepdims=True)


def partial_kernel(q_ref, k_ref, v_ref, o_ref, m_ref, l_ref):
    rows = q_ref.shape[0]
    diagonal = lax.broadcasted_iota(jnp.int32, (rows, rows), 0) == lax.broadcasted_iota(
        jnp.int32, (rows, rows), 1
    )
    for h in range(HEADS_PER_STEP):
        cols = slice(h * HEAD_DIM, (h + 1) * HEAD_DIM)
        s = lax.dot_general(q_ref[:, cols], k_ref[:, cols], NT_DIMS, preferred_element_type=jnp.float32) * SCALE
        m = jnp.max(s, axis=1, keepdims=True)
        p = jnp.exp(s - m)
        total = jnp.sum(p, axis=1, keepdims=True)
        mixed = jnp.dot(p.astype(jnp.bfloat16), v_ref[:, cols], preferred_element_type=jnp.float32)
        o_ref[:, cols] = mixed.astype(o_ref.dtype)
        m_ref[h : h + 1, :] = column_to_row(m, diagonal)
        l_ref[h : h + 1, :] = column_to_row(total, diagonal)


def final_kernel(block_ref, q_ref, k_ref, v_ref, kp_ref, vp_ref, o_ref, m_ref, l_ref, *rest):
    out_ref, lse_ref = rest[-2:]
    block_index = block_ref[0]
    rows = q_ref.shape[0]
    row_id = lax.broadcasted_iota(jnp.int32, (rows, rows), 0)
    col_id = lax.broadcasted_iota(jnp.int32, (rows, rows), 1)
    causal = col_id <= row_id
    diagonal = col_id == row_id
    has_prev = block_index >= 1
    has_prev2 = block_index >= 2
    for h in range(HEADS_PER_STEP):
        cols = slice(h * HEAD_DIM, (h + 1) * HEAD_DIM)
        q = q_ref[:, cols]
        s_own = lax.dot_general(q, k_ref[:, cols], NT_DIMS, preferred_element_type=jnp.float32) * SCALE
        s_prev = lax.dot_general(q, kp_ref[:, cols], NT_DIMS, preferred_element_type=jnp.float32) * SCALE
        s_own = jnp.where(causal, s_own, -jnp.inf)
        s_prev = jnp.where(has_prev, s_prev, -jnp.inf)
        m_far = row_to_column(m_ref[h : h + 1, :], diagonal)
        l_far = row_to_column(l_ref[h : h + 1, :], diagonal)
        m_near = jnp.maximum(jnp.max(s_own, axis=1, keepdims=True), jnp.max(s_prev, axis=1, keepdims=True))
        m = jnp.where(has_prev2, jnp.maximum(m_near, m_far), m_near)
        far_scale = jnp.where(has_prev2, jnp.exp(m_far - m), 0.0)
        p_own = jnp.exp(s_own - m)
        p_prev = jnp.exp(s_prev - m)
        total = (
            jnp.sum(p_own, axis=1, keepdims=True)
            + jnp.sum(p_prev, axis=1, keepdims=True)
            + jnp.where(has_prev2, far_scale * l_far, 0.0)
        )
        mixed = (
            jnp.dot(p_own.astype(jnp.bfloat16), v_ref[:, cols], preferred_element_type=jnp.float32)
            + jnp.dot(p_prev.astype(jnp.bfloat16), vp_ref[:, cols], preferred_element_type=jnp.float32)
            + jnp.where(has_prev2, far_scale * o_ref[:, cols].astype(jnp.float32), 0.0)
        )
        out_ref[:, cols] = (mixed / total).astype(out_ref.dtype)
        lse_ref[h : h + 1, :] = column_to_row(m + jnp.log(total), diagonal)


def partial_attention(q, k, v):
    rows, width = q.shape
    step_width = HEADS_PER_STEP * HEAD_DIM
    steps = width // step_width
    block = pl.BlockSpec((rows, step_width), lambda g: (0, g))
    stat = pl.BlockSpec((HEADS_PER_STEP, rows), lambda g: (g, 0))
    return pl.pallas_call(
        partial_kernel,
        grid=(steps,),
        in_specs=[block] * 3,
        out_specs=[block, stat, stat],
        out_shape=[
            jax.ShapeDtypeStruct((rows, width), jnp.bfloat16),
            jax.ShapeDtypeStruct((width // HEAD_DIM, rows), jnp.float32),
            jax.ShapeDtypeStruct((width // HEAD_DIM, rows), jnp.float32),
        ],
    )(q, k, v)


def final_attention(block_index, chunk, q, k, v, k_prev, v_prev, o_far, m_far, l_far, previous):
    rows, width = q.shape
    step_width = HEADS_PER_STEP * HEAD_DIM
    steps = k_prev.shape[1] // step_width
    offset = chunk * steps
    whole = pl.BlockSpec((rows, step_width), lambda g, b: (0, g + offset))
    part = pl.BlockSpec((rows, step_width), lambda g, b: (0, g))
    stat = pl.BlockSpec((HEADS_PER_STEP, rows), lambda g, b: (g, 0))
    out_stat = pl.BlockSpec((HEADS_PER_STEP, rows), lambda g, b: (g + offset, 0))
    operands = [block_index, q, k, v, k_prev, v_prev, o_far, m_far, l_far]
    in_specs = [whole] * 3 + [part] * 3 + [stat] * 2
    aliases = {}
    if previous is not None:
        in_specs = in_specs + [pl.BlockSpec(memory_space=pl.ANY)] * 2
        aliases = {len(operands): 0, len(operands) + 1: 1}
        operands = operands + list(previous)
    return pl.pallas_call(
        final_kernel,
        grid_spec=pltpu.PrefetchScalarGridSpec(
            num_scalar_prefetch=1,
            grid=(steps,),
            in_specs=in_specs,
            out_specs=[whole, out_stat],
        ),
        out_shape=[
            jax.ShapeDtypeStruct((rows, width), jnp.bfloat16),
            jax.ShapeDtypeStruct((width // HEAD_DIM, rows), jnp.float32),
        ],
        input_output_aliases=aliases,
    )(*operands)


def shards(att_query, att_key, att_value):
    width = att_query.shape[1]
    chunk_width = width // CHUNKS
    block_index = lax.axis_index("ctx").astype(jnp.int32).reshape(1)
    arrivals = []
    for chunk in range(CHUNKS):
        cols = slice(chunk * chunk_width, (chunk + 1) * chunk_width)
        k_prev, v_prev = from_behind((att_key[:, cols], att_value[:, cols]), "ctx")
        q_next = from_ahead(att_query[:, cols], "ctx")
        far = partial_attention(q_next, k_prev, v_prev)
        o_far, m_far, l_far = from_behind(far, "ctx")
        arrivals.append((k_prev, v_prev, o_far, m_far, l_far))
    result = None
    for chunk in range(CHUNKS):
        result = final_attention(
            block_index, chunk, att_query, att_key, att_value, *arrivals[chunk], result
        )
    return tuple(result)


def solution(mesh):
    return jax.shard_map(
        shards,
        mesh=mesh,
        in_specs=(P(("dp", "ctx"), None), P(("dp", "ctx"), None), P(("dp", "ctx"), None)),
        out_specs=(P(("dp", "ctx"), None), P(None, ("dp", "ctx"))),
        check_vma=False,
    )
```

```python
import math

import jax
import jax.numpy as jnp
from jax import lax
from jax.experimental import pallas as pl
from jax.experimental.pallas import tpu as pltpu
from jax.sharding import PartitionSpec as P

HEAD_DIM = 128
HEADS_PER_STEP = 8
CHUNKS = 2
SCALE = 1.0 / math.sqrt(HEAD_DIM)
NT_DIMS = (((1,), (1,)), ((), ()))


def from_behind(block, axis):
    devices = range(lax.axis_size(axis))
    route = [(i - 1, i) for i in devices if i - 1 in devices]
    return lax.ppermute(block, axis, route)


def from_ahead(block, axis):
    devices = range(lax.axis_size(axis))
    route = [(i + 1, i) for i in devices if i + 1 in devices]
    return lax.ppermute(block, axis, route)


def scores(q, k):
    return lax.dot_general(q, k, NT_DIMS, preferred_element_type=jnp.float32) * SCALE


def row_sums(weights, ones):
    return jnp.dot(weights, ones, preferred_element_type=jnp.float32)


def partial_kernel(q_ref, k_ref, v_ref, o_ref, stat_ref):
    rows = q_ref.shape[0]
    ones = jnp.ones((rows, HEAD_DIM), jnp.bfloat16)
    for h in range(HEADS_PER_STEP):
        cols = slice(h * HEAD_DIM, (h + 1) * HEAD_DIM)
        s = scores(q_ref[:, cols], k_ref[:, cols])
        m = jnp.max(s, axis=1, keepdims=True)
        p = jnp.exp(s - m).astype(jnp.bfloat16)
        o_ref[:, cols] = jnp.dot(p, v_ref[:, cols], preferred_element_type=jnp.float32).astype(o_ref.dtype)
        stat_ref[:, h : h + 1] = m
        stat_ref[:, HEADS_PER_STEP + h : HEADS_PER_STEP + h + 1] = row_sums(p, ones)[:, 0:1]


def final_kernel(block_ref, q_ref, k_ref, v_ref, kp_ref, vp_ref, o_ref, stat_ref, *rest):
    out_ref, lse_ref = rest[-2:]
    block_index = block_ref[0]
    rows = q_ref.shape[0]
    row_id = lax.broadcasted_iota(jnp.int32, (rows, rows), 0)
    col_id = lax.broadcasted_iota(jnp.int32, (rows, rows), 1)
    causal = col_id <= row_id
    diagonal = col_id == row_id
    has_prev = block_index >= 1
    has_prev2 = block_index >= 2
    ones = jnp.ones((rows, HEAD_DIM), jnp.bfloat16)
    for h in range(HEADS_PER_STEP):
        cols = slice(h * HEAD_DIM, (h + 1) * HEAD_DIM)
        q = q_ref[:, cols]
        s_own = jnp.where(causal, scores(q, k_ref[:, cols]), -jnp.inf)
        s_prev = jnp.where(has_prev, scores(q, kp_ref[:, cols]), -jnp.inf)
        m_near = jnp.max(jnp.maximum(s_own, s_prev), axis=1, keepdims=True)
        m_far = stat_ref[:, h : h + 1]
        l_far = stat_ref[:, HEADS_PER_STEP + h : HEADS_PER_STEP + h + 1]
        m = jnp.where(has_prev2, jnp.maximum(m_near, m_far), m_near)
        far_scale = jnp.where(has_prev2, jnp.exp(m_far - m), 0.0)
        p_own = jnp.exp(s_own - m).astype(jnp.bfloat16)
        p_prev = jnp.exp(s_prev - m).astype(jnp.bfloat16)
        total = row_sums(p_own, ones) + row_sums(p_prev, ones) + far_scale * l_far
        mixed = (
            jnp.dot(p_own, v_ref[:, cols], preferred_element_type=jnp.float32)
            + jnp.dot(p_prev, vp_ref[:, cols], preferred_element_type=jnp.float32)
            + far_scale * o_ref[:, cols].astype(jnp.float32)
        )
        out_ref[:, cols] = (mixed / total).astype(out_ref.dtype)
        lse = m + jnp.log(total[:, 0:1])
        lse_ref[h : h + 1, :] = jnp.sum(jnp.where(diagonal, lse, 0.0), axis=0, keepdims=True)


def partial_attention(q, kv):
    rows, width = q.shape
    step_width = HEADS_PER_STEP * HEAD_DIM
    steps = width // step_width
    block = pl.BlockSpec((rows, step_width), lambda g: (0, g))
    key_block = pl.BlockSpec((None, rows, step_width), lambda g: (0, 0, g))
    value_block = pl.BlockSpec((None, rows, step_width), lambda g: (1, 0, g))
    stat = pl.BlockSpec((None, rows, 2 * HEADS_PER_STEP), lambda g: (g, 0, 0))
    return pl.pallas_call(
        partial_kernel,
        grid=(steps,),
        in_specs=[block, key_block, value_block],
        out_specs=[block, stat],
        out_shape=[
            jax.ShapeDtypeStruct((rows, width), jnp.bfloat16),
            jax.ShapeDtypeStruct((steps, rows, 2 * HEADS_PER_STEP), jnp.float32),
        ],
    )(q, kv, kv)


def final_attention(block_index, chunk, q, k, v, kv_prev, o_far, stat_far, previous):
    rows, width = q.shape
    step_width = HEADS_PER_STEP * HEAD_DIM
    steps = o_far.shape[1] // step_width
    offset = chunk * steps
    whole = pl.BlockSpec((rows, step_width), lambda g, b: (0, g + offset))
    part = pl.BlockSpec((rows, step_width), lambda g, b: (0, g))
    key_block = pl.BlockSpec((None, rows, step_width), lambda g, b: (0, 0, g))
    value_block = pl.BlockSpec((None, rows, step_width), lambda g, b: (1, 0, g))
    stat = pl.BlockSpec((None, rows, 2 * HEADS_PER_STEP), lambda g, b: (g, 0, 0))
    out_stat = pl.BlockSpec((HEADS_PER_STEP, rows), lambda g, b: (g + offset, 0))
    operands = [block_index, q, k, v, kv_prev, kv_prev, o_far, stat_far]
    in_specs = [whole] * 3 + [key_block, value_block, part, stat]
    aliases = {}
    if previous is not None:
        in_specs = in_specs + [pl.BlockSpec(memory_space=pl.ANY)] * 2
        aliases = {len(operands): 0, len(operands) + 1: 1}
        operands = operands + list(previous)
    return pl.pallas_call(
        final_kernel,
        grid_spec=pltpu.PrefetchScalarGridSpec(
            num_scalar_prefetch=1,
            grid=(steps,),
            in_specs=in_specs,
            out_specs=[whole, out_stat],
        ),
        out_shape=[
            jax.ShapeDtypeStruct((rows, width), jnp.bfloat16),
            jax.ShapeDtypeStruct((width // HEAD_DIM, rows), jnp.float32),
        ],
        input_output_aliases=aliases,
    )(*operands)


def shards(att_query, att_key, att_value):
    width = att_query.shape[1]
    chunk_width = width // CHUNKS
    block_index = lax.axis_index("ctx").astype(jnp.int32).reshape(1)
    arrivals = []
    for chunk in range(CHUNKS):
        cols = slice(chunk * chunk_width, (chunk + 1) * chunk_width)
        kv_prev = from_behind(jnp.stack([att_key[:, cols], att_value[:, cols]]), "ctx")
        q_next = from_ahead(att_query[:, cols], "ctx")
        o_far, stat_far = from_behind(partial_attention(q_next, kv_prev), "ctx")
        arrivals.append((kv_prev, o_far, stat_far))
    result = None
    for chunk in range(CHUNKS):
        result = final_attention(block_index, chunk, att_query, att_key, att_value, *arrivals[chunk], result)
    return tuple(result)


def solution(mesh):
    return jax.shard_map(
        shards,
        mesh=mesh,
        in_specs=(P(("dp", "ctx"), None), P(("dp", "ctx"), None), P(("dp", "ctx"), None)),
        out_specs=(P(("dp", "ctx"), None), P(None, ("dp", "ctx"))),
        check_vma=False,
    )
```

```python
import math

import jax
import jax.numpy as jnp
from jax import lax
from jax.experimental import pallas as pl
from jax.experimental.pallas import tpu as pltpu
from jax.sharding import PartitionSpec as P

HEAD_DIM = 128
HEADS_PER_STEP = 8
SCALE = 1.0 / math.sqrt(HEAD_DIM)
NT_DIMS = (((1,), (1,)), ((), ()))


def from_behind(block, axis):
    devices = range(lax.axis_size(axis))
    route = [(i - 1, i) for i in devices if i - 1 in devices]
    return lax.ppermute(block, axis, route)


def from_ahead(block, axis):
    devices = range(lax.axis_size(axis))
    route = [(i + 1, i) for i in devices if i + 1 in devices]
    return lax.ppermute(block, axis, route)


def weighted_values(weights, values):
    ones = jnp.ones((values.shape[0], HEAD_DIM), values.dtype)
    result = jnp.dot(weights, jnp.concatenate([values, ones], axis=1), preferred_element_type=jnp.float32)
    return result[:, :HEAD_DIM], result[:, HEAD_DIM : HEAD_DIM + 1]


def partial_kernel(q_ref, k_ref, v_ref, o_ref, stat_ref):
    for h in range(HEADS_PER_STEP):
        cols = slice(h * HEAD_DIM, (h + 1) * HEAD_DIM)
        s = lax.dot_general(q_ref[:, cols], k_ref[:, cols], NT_DIMS, preferred_element_type=jnp.float32) * SCALE
        m = jnp.max(s, axis=1, keepdims=True)
        p = jnp.exp(s - m).astype(jnp.bfloat16)
        mixed, total = weighted_values(p, v_ref[:, cols])
        o_ref[:, cols] = mixed.astype(o_ref.dtype)
        stat_ref[:, h : h + 1] = m
        stat_ref[:, HEADS_PER_STEP + h : HEADS_PER_STEP + h + 1] = total


def near_kernel(block_ref, q_ref, k_ref, v_ref, kp_ref, vp_ref, mixed_ref, stat_ref):
    rows = q_ref.shape[0]
    row_id = lax.broadcasted_iota(jnp.int32, (rows, 2 * rows), 0)
    col_id = lax.broadcasted_iota(jnp.int32, (rows, 2 * rows), 1)
    first_prev = jnp.where(block_ref[0] >= 1, rows, 2 * rows)
    allowed = (col_id <= row_id) | (col_id >= first_prev)
    for h in range(HEADS_PER_STEP):
        cols = slice(h * HEAD_DIM, (h + 1) * HEAD_DIM)
        keys = jnp.concatenate([k_ref[:, cols], kp_ref[:, cols]], axis=0)
        values = jnp.concatenate([v_ref[:, cols], vp_ref[:, cols]], axis=0)
        s = lax.dot_general(q_ref[:, cols], keys, NT_DIMS, preferred_element_type=jnp.float32) * SCALE
        s = jnp.where(allowed, s, -jnp.inf)
        m = jnp.max(s, axis=1, keepdims=True)
        p = jnp.exp(s - m).astype(jnp.bfloat16)
        mixed, total = weighted_values(p, values)
        mixed_ref[:, cols] = mixed
        stat_ref[:, h : h + 1] = m
        stat_ref[:, HEADS_PER_STEP + h : HEADS_PER_STEP + h + 1] = total


def stat_spec(rows):
    return pl.BlockSpec((None, rows, 2 * HEADS_PER_STEP), lambda g, *_: (g, 0, 0))


def partial_attention(q, kv):
    rows, width = q.shape
    step_width = HEADS_PER_STEP * HEAD_DIM
    steps = width // step_width
    block = pl.BlockSpec((rows, step_width), lambda g: (0, g))
    key_block = pl.BlockSpec((None, rows, step_width), lambda g: (0, 0, g))
    value_block = pl.BlockSpec((None, rows, step_width), lambda g: (1, 0, g))
    return pl.pallas_call(
        partial_kernel,
        grid=(steps,),
        in_specs=[block, key_block, value_block],
        out_specs=[block, stat_spec(rows)],
        out_shape=[
            jax.ShapeDtypeStruct((rows, width), jnp.bfloat16),
            jax.ShapeDtypeStruct((steps, rows, 2 * HEADS_PER_STEP), jnp.float32),
        ],
    )(q, kv, kv)


def near_attention(block_index, q, k, v, kv_prev):
    rows, width = q.shape
    step_width = HEADS_PER_STEP * HEAD_DIM
    steps = width // step_width
    block = pl.BlockSpec((rows, step_width), lambda g, b: (0, g))
    key_block = pl.BlockSpec((None, rows, step_width), lambda g, b: (0, 0, g))
    value_block = pl.BlockSpec((None, rows, step_width), lambda g, b: (1, 0, g))
    return pl.pallas_call(
        near_kernel,
        grid_spec=pltpu.PrefetchScalarGridSpec(
            num_scalar_prefetch=1,
            grid=(steps,),
            in_specs=[block] * 3 + [key_block, value_block],
            out_specs=[block, stat_spec(rows)],
        ),
        out_shape=[
            jax.ShapeDtypeStruct((rows, width), jnp.float32),
            jax.ShapeDtypeStruct((steps, rows, 2 * HEADS_PER_STEP), jnp.float32),
        ],
    )(block_index, q, k, v, kv_prev, kv_prev)


def per_head(stat):
    steps, rows, _ = stat.shape
    stat = jnp.transpose(stat.reshape(steps, rows, 2, HEADS_PER_STEP), (2, 1, 0, 3))
    return stat[0].reshape(rows, steps * HEADS_PER_STEP), stat[1].reshape(rows, steps * HEADS_PER_STEP)


def merge(block_index, mixed_near, stat_near, o_far, stat_far):
    rows, width = mixed_near.shape
    heads = width // HEAD_DIM
    m_near, l_near = per_head(stat_near)
    m_far, l_far = per_head(stat_far)
    has_far = block_index >= 2
    m = jnp.where(has_far, jnp.maximum(m_near, m_far), m_near)
    near_scale = jnp.exp(m_near - m)
    far_scale = jnp.where(has_far, jnp.exp(m_far - m), 0.0)
    total = near_scale * l_near + far_scale * l_far
    mixed = (
        near_scale[:, :, None] * mixed_near.reshape(rows, heads, HEAD_DIM)
        + far_scale[:, :, None] * o_far.reshape(rows, heads, HEAD_DIM).astype(jnp.float32)
    )
    out = (mixed / total[:, :, None]).reshape(rows, width).astype(jnp.bfloat16)
    return out, jnp.transpose(m + jnp.log(total))


def shards(att_query, att_key, att_value):
    block_index = lax.axis_index("ctx").astype(jnp.int32)
    kv_prev = from_behind(jnp.stack([att_key, att_value]), "ctx")
    q_next = from_ahead(att_query, "ctx")
    o_far, stat_far = from_behind(partial_attention(q_next, kv_prev), "ctx")
    mixed_near, stat_near = near_attention(block_index.reshape(1), att_query, att_key, att_value, kv_prev)
    return merge(block_index, mixed_near, stat_near, o_far, stat_far)


def solution(mesh):
    return jax.shard_map(
        shards,
        mesh=mesh,
        in_specs=(P(("dp", "ctx"), None), P(("dp", "ctx"), None), P(("dp", "ctx"), None)),
        out_specs=(P(("dp", "ctx"), None), P(None, ("dp", "ctx"))),
        check_vma=False,
    )
```

```python
import math

import jax
import jax.numpy as jnp
from jax import lax
from jax.experimental import pallas as pl
from jax.experimental.pallas import tpu as pltpu
from jax.sharding import PartitionSpec as P

HEAD_DIM = 128
HEADS_PER_STEP = 8
CHUNKS = 2
SCALE = 1.0 / math.sqrt(HEAD_DIM)
NT_DIMS = (((1,), (1,)), ((), ()))


def from_behind(block, axis):
    devices = range(lax.axis_size(axis))
    route = [(i - 1, i) for i in devices if i - 1 in devices]
    return lax.ppermute(block, axis, route)


def from_ahead(block, axis):
    devices = range(lax.axis_size(axis))
    route = [(i + 1, i) for i in devices if i + 1 in devices]
    return lax.ppermute(block, axis, route)


def weighted_values(weights, values):
    ones = jnp.ones((values.shape[0], HEAD_DIM), values.dtype)
    result = jnp.dot(weights, jnp.concatenate([values, ones], axis=1), preferred_element_type=jnp.float32)
    return result[:, :HEAD_DIM], result[:, HEAD_DIM : HEAD_DIM + 1]


def partial_kernel(q_ref, k_ref, v_ref, *rest):
    o_ref, stat_ref = rest[-2:]
    ones = jnp.ones((q_ref.shape[0], HEAD_DIM), jnp.bfloat16)
    for h in range(HEADS_PER_STEP):
        cols = slice(h * HEAD_DIM, (h + 1) * HEAD_DIM)
        s = lax.dot_general(q_ref[:, cols], k_ref[:, cols], NT_DIMS, preferred_element_type=jnp.float32) * SCALE
        m = jnp.max(s, axis=1, keepdims=True)
        p = jnp.exp(s - m).astype(jnp.bfloat16)
        o_ref[:, cols] = jnp.dot(p, v_ref[:, cols], preferred_element_type=jnp.float32).astype(o_ref.dtype)
        stat_ref[:, h : h + 1] = m
        total = jnp.dot(p, ones, preferred_element_type=jnp.float32)
        stat_ref[:, HEADS_PER_STEP + h : HEADS_PER_STEP + h + 1] = total[:, 0:1]


def near_kernel(block_ref, q_ref, k_ref, v_ref, kp_ref, vp_ref, mixed_ref, stat_ref):
    rows = q_ref.shape[0]
    row_id = lax.broadcasted_iota(jnp.int32, (rows, 2 * rows), 0)
    col_id = lax.broadcasted_iota(jnp.int32, (rows, 2 * rows), 1)
    first_prev = jnp.where(block_ref[0] >= 1, rows, 2 * rows)
    allowed = (col_id <= row_id) | (col_id >= first_prev)
    for h in range(HEADS_PER_STEP):
        cols = slice(h * HEAD_DIM, (h + 1) * HEAD_DIM)
        keys = jnp.concatenate([k_ref[:, cols], kp_ref[:, cols]], axis=0)
        values = jnp.concatenate([v_ref[:, cols], vp_ref[:, cols]], axis=0)
        s = lax.dot_general(q_ref[:, cols], keys, NT_DIMS, preferred_element_type=jnp.float32) * SCALE
        s = jnp.where(allowed, s, -jnp.inf)
        m = jnp.max(s, axis=1, keepdims=True)
        p = jnp.exp(s - m).astype(jnp.bfloat16)
        mixed, total = weighted_values(p, values)
        mixed_ref[:, cols] = mixed
        stat_ref[:, h : h + 1] = m
        stat_ref[:, HEADS_PER_STEP + h : HEADS_PER_STEP + h + 1] = total


def stat_spec(rows):
    return pl.BlockSpec((None, rows, 2 * HEADS_PER_STEP), lambda g, *_: (g, 0, 0))


def partial_attention(q, kv, after=()):
    rows, width = q.shape
    step_width = HEADS_PER_STEP * HEAD_DIM
    steps = width // step_width
    block = pl.BlockSpec((rows, step_width), lambda g: (0, g))
    key_block = pl.BlockSpec((None, rows, step_width), lambda g: (0, 0, g))
    value_block = pl.BlockSpec((None, rows, step_width), lambda g: (1, 0, g))
    return pl.pallas_call(
        partial_kernel,
        grid=(steps,),
        in_specs=[block, key_block, value_block] + [pl.BlockSpec(memory_space=pl.ANY)] * len(after),
        out_specs=[block, stat_spec(rows)],
        out_shape=[
            jax.ShapeDtypeStruct((rows, width), jnp.bfloat16),
            jax.ShapeDtypeStruct((steps, rows, 2 * HEADS_PER_STEP), jnp.float32),
        ],
    )(q, kv, kv, *after)


def near_attention(block_index, q, k, v, kv_prev):
    rows, width = q.shape
    step_width = HEADS_PER_STEP * HEAD_DIM
    steps = width // step_width
    block = pl.BlockSpec((rows, step_width), lambda g, b: (0, g))
    key_block = pl.BlockSpec((None, rows, step_width), lambda g, b: (0, 0, g))
    value_block = pl.BlockSpec((None, rows, step_width), lambda g, b: (1, 0, g))
    return pl.pallas_call(
        near_kernel,
        grid_spec=pltpu.PrefetchScalarGridSpec(
            num_scalar_prefetch=1,
            grid=(steps,),
            in_specs=[block] * 3 + [key_block, value_block],
            out_specs=[block, stat_spec(rows)],
        ),
        out_shape=[
            jax.ShapeDtypeStruct((rows, width), jnp.float32),
            jax.ShapeDtypeStruct((steps, rows, 2 * HEADS_PER_STEP), jnp.float32),
        ],
    )(block_index, q, k, v, kv_prev, kv_prev)


def merge_kernel(block_ref, mixed_ref, near_ref, o_ref, far_ref, *rest):
    out_ref = rest[-1]
    has_far = block_ref[0] >= 2
    for h in range(HEADS_PER_STEP):
        cols = slice(h * HEAD_DIM, (h + 1) * HEAD_DIM)
        m_near = near_ref[:, h : h + 1]
        m_far = far_ref[:, h : h + 1]
        l_near = near_ref[:, HEADS_PER_STEP + h : HEADS_PER_STEP + h + 1]
        l_far = far_ref[:, HEADS_PER_STEP + h : HEADS_PER_STEP + h + 1]
        m = jnp.where(has_far, jnp.maximum(m_near, m_far), m_near)
        near_scale = jnp.exp(m_near - m)
        far_scale = jnp.where(has_far, jnp.exp(m_far - m), 0.0)
        total = near_scale * l_near + far_scale * l_far
        mixed = near_scale * mixed_ref[:, cols] + far_scale * o_ref[:, cols].astype(jnp.float32)
        out_ref[:, cols] = (mixed / total).astype(out_ref.dtype)


def merged_output(block_index, chunk, width, mixed_near, stat_near, o_far, stat_far, previous):
    rows, chunk_width = mixed_near.shape
    step_width = HEADS_PER_STEP * HEAD_DIM
    steps = chunk_width // step_width
    offset = chunk * steps
    part = pl.BlockSpec((rows, step_width), lambda g, b: (0, g))
    whole = pl.BlockSpec((rows, step_width), lambda g, b: (0, g + offset))
    operands = [block_index, mixed_near, stat_near, o_far, stat_far]
    in_specs = [part, stat_spec(rows), part, stat_spec(rows)]
    aliases = {}
    if previous is not None:
        in_specs = in_specs + [pl.BlockSpec(memory_space=pl.ANY)]
        aliases = {len(operands): 0}
        operands = operands + [previous]
    return pl.pallas_call(
        merge_kernel,
        grid_spec=pltpu.PrefetchScalarGridSpec(
            num_scalar_prefetch=1,
            grid=(steps,),
            in_specs=in_specs,
            out_specs=whole,
        ),
        out_shape=jax.ShapeDtypeStruct((rows, width), jnp.bfloat16),
        input_output_aliases=aliases,
    )(*operands)


def per_head(stat):
    steps, rows, _ = stat.shape
    stat = jnp.transpose(stat.reshape(steps, rows, 2, HEADS_PER_STEP), (2, 1, 0, 3))
    return stat[0].reshape(rows, steps * HEADS_PER_STEP), stat[1].reshape(rows, steps * HEADS_PER_STEP)


def log_total(block_index, stat_near, stat_far):
    m_near, l_near = per_head(stat_near)
    m_far, l_far = per_head(stat_far)
    has_far = block_index >= 2
    m = jnp.where(has_far, jnp.maximum(m_near, m_far), m_near)
    total = jnp.exp(m_near - m) * l_near + jnp.where(has_far, jnp.exp(m_far - m), 0.0) * l_far
    return jnp.transpose(m + jnp.log(total))


def shards(att_query, att_key, att_value):
    width = att_query.shape[1]
    chunk_width = width // CHUNKS
    block_index = lax.axis_index("ctx").astype(jnp.int32)
    index_ref = block_index.reshape(1)
    pieces = []
    for chunk in range(CHUNKS):
        cols = slice(chunk * chunk_width, (chunk + 1) * chunk_width)
        q, k, v = att_query[:, cols], att_key[:, cols], att_value[:, cols]
        kv_prev = from_behind(jnp.stack([k, v]), "ctx")
        q_next = from_ahead(q, "ctx")
        after = (pieces[-1][1], pieces[-1][3]) if pieces else ()
        o_far, stat_far = from_behind(partial_attention(q_next, kv_prev, after), "ctx")
        mixed_near, stat_near = near_attention(index_ref, q, k, v, kv_prev)
        pieces.append((mixed_near, stat_near, o_far, stat_far))
    out = None
    for chunk in range(CHUNKS):
        out = merged_output(index_ref, chunk, width, *pieces[chunk], out)
    stat_near = jnp.concatenate([piece[1] for piece in pieces], axis=0)
    stat_far = jnp.concatenate([piece[3] for piece in pieces], axis=0)
    return out, log_total(block_index, stat_near, stat_far)


def solution(mesh):
    return jax.shard_map(
        shards,
        mesh=mesh,
        in_specs=(P(("dp", "ctx"), None), P(("dp", "ctx"), None), P(("dp", "ctx"), None)),
        out_specs=(P(("dp", "ctx"), None), P(None, ("dp", "ctx"))),
        check_vma=False,
    )
```

```python
import math

import jax
import jax.numpy as jnp
from jax import lax
from jax.experimental import pallas as pl
from jax.experimental.pallas import tpu as pltpu
from jax.sharding import PartitionSpec as P

HEAD_DIM = 128
HEADS_PER_STEP = 8
CHUNKS = 2
SCALE = 1.0 / math.sqrt(HEAD_DIM)
NT_DIMS = (((1,), (1,)), ((), ()))


def from_behind(block, axis):
    devices = range(lax.axis_size(axis))
    route = [(i - 1, i) for i in devices if i - 1 in devices]
    return lax.ppermute(block, axis, route)


def from_ahead(block, axis):
    devices = range(lax.axis_size(axis))
    route = [(i + 1, i) for i in devices if i + 1 in devices]
    return lax.ppermute(block, axis, route)


def weighted_values(weights, values):
    ones = jnp.ones((values.shape[0], HEAD_DIM), values.dtype)
    result = jnp.dot(weights, jnp.concatenate([values, ones], axis=1), preferred_element_type=jnp.float32)
    return result[:, :HEAD_DIM], result[:, HEAD_DIM : HEAD_DIM + 1]


def partial_kernel(q_ref, k_ref, v_ref, *rest):
    o_ref, stat_ref = rest[-2:]
    ones = jnp.ones((q_ref.shape[0], HEAD_DIM), jnp.bfloat16)
    for h in range(HEADS_PER_STEP):
        cols = slice(h * HEAD_DIM, (h + 1) * HEAD_DIM)
        s = lax.dot_general(q_ref[:, cols], k_ref[:, cols], NT_DIMS, preferred_element_type=jnp.float32) * SCALE
        m = jnp.max(s, axis=1, keepdims=True)
        p = jnp.exp(s - m).astype(jnp.bfloat16)
        o_ref[:, cols] = jnp.dot(p, v_ref[:, cols], preferred_element_type=jnp.float32).astype(o_ref.dtype)
        stat_ref[:, h : h + 1] = m
        total = jnp.dot(p, ones, preferred_element_type=jnp.float32)
        stat_ref[:, HEADS_PER_STEP + h : HEADS_PER_STEP + h + 1] = total[:, 0:1]


def near_kernel(block_ref, q_ref, k_ref, v_ref, kp_ref, vp_ref, mixed_ref, stat_ref):
    rows = q_ref.shape[0]
    row_id = lax.broadcasted_iota(jnp.int32, (rows, 2 * rows), 0)
    col_id = lax.broadcasted_iota(jnp.int32, (rows, 2 * rows), 1)
    first_prev = jnp.where(block_ref[0] >= 1, rows, 2 * rows)
    allowed = (col_id <= row_id) | (col_id >= first_prev)
    for h in range(HEADS_PER_STEP):
        cols = slice(h * HEAD_DIM, (h + 1) * HEAD_DIM)
        keys = jnp.concatenate([k_ref[:, cols], kp_ref[:, cols]], axis=0)
        values = jnp.concatenate([v_ref[:, cols], vp_ref[:, cols]], axis=0)
        s = lax.dot_general(q_ref[:, cols], keys, NT_DIMS, preferred_element_type=jnp.float32) * SCALE
        s = jnp.where(allowed, s, -jnp.inf)
        m = jnp.max(s, axis=1, keepdims=True)
        p = jnp.exp(s - m).astype(jnp.bfloat16)
        mixed, total = weighted_values(p, values)
        mixed_ref[:, cols] = mixed
        stat_ref[:, h : h + 1] = m
        stat_ref[:, HEADS_PER_STEP + h : HEADS_PER_STEP + h + 1] = total


def stat_spec(rows):
    return pl.BlockSpec((None, rows, 2 * HEADS_PER_STEP), lambda g, *_: (g, 0, 0))


def partial_attention(q, kv, after=()):
    rows, width = q.shape
    step_width = HEADS_PER_STEP * HEAD_DIM
    steps = width // step_width
    block = pl.BlockSpec((rows, step_width), lambda g: (0, g))
    key_block = pl.BlockSpec((None, rows, step_width), lambda g: (0, 0, g))
    value_block = pl.BlockSpec((None, rows, step_width), lambda g: (1, 0, g))
    return pl.pallas_call(
        partial_kernel,
        grid=(steps,),
        in_specs=[block, key_block, value_block] + [pl.BlockSpec(memory_space=pl.ANY)] * len(after),
        out_specs=[block, stat_spec(rows)],
        out_shape=[
            jax.ShapeDtypeStruct((rows, width), jnp.bfloat16),
            jax.ShapeDtypeStruct((steps, rows, 2 * HEADS_PER_STEP), jnp.float32),
        ],
    )(q, kv, kv, *after)


def near_attention(block_index, q, k, v, kv_prev):
    rows, width = q.shape
    step_width = HEADS_PER_STEP * HEAD_DIM
    steps = width // step_width
    block = pl.BlockSpec((rows, step_width), lambda g, b: (0, g))
    key_block = pl.BlockSpec((None, rows, step_width), lambda g, b: (0, 0, g))
    value_block = pl.BlockSpec((None, rows, step_width), lambda g, b: (1, 0, g))
    return pl.pallas_call(
        near_kernel,
        grid_spec=pltpu.PrefetchScalarGridSpec(
            num_scalar_prefetch=1,
            grid=(steps,),
            in_specs=[block] * 3 + [key_block, value_block],
            out_specs=[block, stat_spec(rows)],
        ),
        out_shape=[
            jax.ShapeDtypeStruct((rows, width), jnp.float32),
            jax.ShapeDtypeStruct((steps, rows, 2 * HEADS_PER_STEP), jnp.float32),
        ],
    )(block_index, q, k, v, kv_prev, kv_prev)


def merge_kernel(block_ref, mixed_ref, near_ref, o_ref, far_ref, *rest):
    out_ref = rest[-1]
    has_far = block_ref[0] >= 2
    n = HEADS_PER_STEP
    near = near_ref[...]
    far = far_ref[...]
    m_near, l_near = near[:, :n], near[:, n:]
    m_far, l_far = far[:, :n], far[:, n:]
    m = jnp.where(has_far, jnp.maximum(m_near, m_far), m_near)
    near_scale = jnp.exp(m_near - m)
    far_scale = jnp.where(has_far, jnp.exp(m_far - m), 0.0)
    inverse = 1.0 / (near_scale * l_near + far_scale * l_far)
    near_scale = near_scale * inverse
    far_scale = far_scale * inverse
    for h in range(n):
        cols = slice(h * HEAD_DIM, (h + 1) * HEAD_DIM)
        mixed = near_scale[:, h : h + 1] * mixed_ref[:, cols] + far_scale[:, h : h + 1] * o_ref[:, cols].astype(
            jnp.float32
        )
        out_ref[:, cols] = mixed.astype(out_ref.dtype)


def merged_output(block_index, chunk, width, mixed_near, stat_near, o_far, stat_far, previous):
    rows, chunk_width = mixed_near.shape
    step_width = HEADS_PER_STEP * HEAD_DIM
    steps = chunk_width // step_width
    offset = chunk * steps
    part = pl.BlockSpec((rows, step_width), lambda g, b: (0, g))
    whole = pl.BlockSpec((rows, step_width), lambda g, b: (0, g + offset))
    operands = [block_index, mixed_near, stat_near, o_far, stat_far]
    in_specs = [part, stat_spec(rows), part, stat_spec(rows)]
    aliases = {}
    if previous is not None:
        in_specs = in_specs + [pl.BlockSpec(memory_space=pl.ANY)]
        aliases = {len(operands): 0}
        operands = operands + [previous]
    return pl.pallas_call(
        merge_kernel,
        grid_spec=pltpu.PrefetchScalarGridSpec(
            num_scalar_prefetch=1,
            grid=(steps,),
            in_specs=in_specs,
            out_specs=whole,
        ),
        out_shape=jax.ShapeDtypeStruct((rows, width), jnp.bfloat16),
        input_output_aliases=aliases,
    )(*operands)


def per_head(stat):
    steps, rows, _ = stat.shape
    stat = jnp.transpose(stat.reshape(steps, rows, 2, HEADS_PER_STEP), (2, 1, 0, 3))
    return stat[0].reshape(rows, steps * HEADS_PER_STEP), stat[1].reshape(rows, steps * HEADS_PER_STEP)


def log_total(block_index, stat_near, stat_far):
    m_near, l_near = per_head(stat_near)
    m_far, l_far = per_head(stat_far)
    has_far = block_index >= 2
    m = jnp.where(has_far, jnp.maximum(m_near, m_far), m_near)
    total = jnp.exp(m_near - m) * l_near + jnp.where(has_far, jnp.exp(m_far - m), 0.0) * l_far
    return jnp.transpose(m + jnp.log(total))


def shards(att_query, att_key, att_value):
    width = att_query.shape[1]
    chunk_width = width // CHUNKS
    block_index = lax.axis_index("ctx").astype(jnp.int32)
    index_ref = block_index.reshape(1)
    pieces = []
    out = None
    for chunk in range(CHUNKS):
        cols = slice(chunk * chunk_width, (chunk + 1) * chunk_width)
        q, k, v = att_query[:, cols], att_key[:, cols], att_value[:, cols]
        kv_prev = from_behind(jnp.stack([k, v]), "ctx")
        q_next = from_ahead(q, "ctx")
        after = (pieces[-1][1], pieces[-1][3]) if pieces else ()
        o_part, stat_part = partial_attention(q_next, kv_prev, after)
        o_far = from_behind(o_part, "ctx")
        mixed_near, stat_near = near_attention(index_ref, q, k, v, kv_prev)
        if pieces:
            out = merged_output(index_ref, chunk - 1, width, *pieces[-1], out)
            stat_part, out = lax.optimization_barrier((stat_part, out))
        stat_far = from_behind(stat_part, "ctx")
        pieces.append((mixed_near, stat_near, o_far, stat_far))
    out = merged_output(index_ref, CHUNKS - 1, width, *pieces[-1], out)
    stat_near = jnp.concatenate([piece[1] for piece in pieces], axis=0)
    stat_far = jnp.concatenate([piece[3] for piece in pieces], axis=0)
    return out, log_total(block_index, stat_near, stat_far)


def solution(mesh):
    return jax.shard_map(
        shards,
        mesh=mesh,
        in_specs=(P(("dp", "ctx"), None), P(("dp", "ctx"), None), P(("dp", "ctx"), None)),
        out_specs=(P(("dp", "ctx"), None), P(None, ("dp", "ctx"))),
        check_vma=False,
    )
```

```python
import math

import jax
import jax.numpy as jnp
from jax import lax
from jax.experimental import pallas as pl
from jax.experimental.pallas import tpu as pltpu
from jax.sharding import PartitionSpec as P

HEAD_DIM = 128
HEADS_PER_STEP = 8
CHUNKS = 2
SCALE = 1.0 / math.sqrt(HEAD_DIM)
NT_DIMS = (((1,), (1,)), ((), ()))


def from_behind(block, axis):
    devices = range(lax.axis_size(axis))
    route = [(i - 1, i) for i in devices if i - 1 in devices]
    return lax.ppermute(block, axis, route)


def from_ahead(block, axis):
    devices = range(lax.axis_size(axis))
    route = [(i + 1, i) for i in devices if i + 1 in devices]
    return lax.ppermute(block, axis, route)


def weighted_values(weights, values):
    ones = jnp.ones((values.shape[0], HEAD_DIM), values.dtype)
    result = jnp.dot(weights, jnp.concatenate([values, ones], axis=1), preferred_element_type=jnp.float32)
    return result[:, :HEAD_DIM], result[:, HEAD_DIM : HEAD_DIM + 1]


def partial_kernel(q_ref, k_ref, v_ref, *rest):
    o_ref, stat_ref = rest[-2:]
    ones = jnp.ones((q_ref.shape[0], HEAD_DIM), jnp.bfloat16)
    for h in range(HEADS_PER_STEP):
        cols = slice(h * HEAD_DIM, (h + 1) * HEAD_DIM)
        s = lax.dot_general(q_ref[:, cols], k_ref[:, cols], NT_DIMS, preferred_element_type=jnp.float32) * SCALE
        m = jnp.max(s, axis=1, keepdims=True)
        p = jnp.exp(s - m).astype(jnp.bfloat16)
        o_ref[:, cols] = jnp.dot(p, v_ref[:, cols], preferred_element_type=jnp.float32).astype(o_ref.dtype)
        stat_ref[:, h : h + 1] = m
        total = jnp.dot(p, ones, preferred_element_type=jnp.float32)
        stat_ref[:, HEADS_PER_STEP + h : HEADS_PER_STEP + h + 1] = total[:, 0:1]


def near_kernel(block_ref, q_ref, k_ref, v_ref, kp_ref, vp_ref, *rest):
    mixed_ref, stat_ref = rest[-2:]
    rows = q_ref.shape[0]
    row_id = lax.broadcasted_iota(jnp.int32, (rows, 2 * rows), 0)
    col_id = lax.broadcasted_iota(jnp.int32, (rows, 2 * rows), 1)
    first_prev = jnp.where(block_ref[0] >= 1, rows, 2 * rows)
    allowed = (col_id <= row_id) | (col_id >= first_prev)
    for h in range(HEADS_PER_STEP):
        cols = slice(h * HEAD_DIM, (h + 1) * HEAD_DIM)
        keys = jnp.concatenate([k_ref[:, cols], kp_ref[:, cols]], axis=0)
        values = jnp.concatenate([v_ref[:, cols], vp_ref[:, cols]], axis=0)
        s = lax.dot_general(q_ref[:, cols], keys, NT_DIMS, preferred_element_type=jnp.float32) * SCALE
        s = jnp.where(allowed, s, -jnp.inf)
        m = jnp.max(s, axis=1, keepdims=True)
        p = jnp.exp(s - m).astype(jnp.bfloat16)
        mixed, total = weighted_values(p, values)
        mixed_ref[:, cols] = mixed
        stat_ref[:, h : h + 1] = m
        stat_ref[:, HEADS_PER_STEP + h : HEADS_PER_STEP + h + 1] = total


def stat_spec(rows):
    return pl.BlockSpec((None, rows, 2 * HEADS_PER_STEP), lambda g, *_: (g, 0, 0))


def partial_attention(q, kv, after=()):
    rows, width = q.shape
    step_width = HEADS_PER_STEP * HEAD_DIM
    steps = width // step_width
    block = pl.BlockSpec((rows, step_width), lambda g: (0, g))
    key_block = pl.BlockSpec((None, rows, step_width), lambda g: (0, 0, g))
    value_block = pl.BlockSpec((None, rows, step_width), lambda g: (1, 0, g))
    return pl.pallas_call(
        partial_kernel,
        grid=(steps,),
        in_specs=[block, key_block, value_block] + [pl.BlockSpec(memory_space=pl.ANY)] * len(after),
        out_specs=[block, stat_spec(rows)],
        out_shape=[
            jax.ShapeDtypeStruct((rows, width), jnp.bfloat16),
            jax.ShapeDtypeStruct((steps, rows, 2 * HEADS_PER_STEP), jnp.float32),
        ],
    )(q, kv, kv, *after)


def near_attention(block_index, q, k, v, kv_prev, after=()):
    rows, width = q.shape
    step_width = HEADS_PER_STEP * HEAD_DIM
    steps = width // step_width
    block = pl.BlockSpec((rows, step_width), lambda g, b: (0, g))
    key_block = pl.BlockSpec((None, rows, step_width), lambda g, b: (0, 0, g))
    value_block = pl.BlockSpec((None, rows, step_width), lambda g, b: (1, 0, g))
    return pl.pallas_call(
        near_kernel,
        grid_spec=pltpu.PrefetchScalarGridSpec(
            num_scalar_prefetch=1,
            grid=(steps,),
            in_specs=[block] * 3 + [key_block, value_block] + [pl.BlockSpec(memory_space=pl.ANY)] * len(after),
            out_specs=[block, stat_spec(rows)],
        ),
        out_shape=[
            jax.ShapeDtypeStruct((rows, width), jnp.float32),
            jax.ShapeDtypeStruct((steps, rows, 2 * HEADS_PER_STEP), jnp.float32),
        ],
    )(block_index, q, k, v, kv_prev, kv_prev, *after)


def merge_kernel(block_ref, mixed_ref, near_ref, o_ref, far_ref, *rest):
    out_ref = rest[-1]
    has_far = block_ref[0] >= 2
    n = HEADS_PER_STEP
    near = near_ref[...]
    far = far_ref[...]
    m_near, l_near = near[:, :n], near[:, n:]
    m_far, l_far = far[:, :n], far[:, n:]
    m = jnp.where(has_far, jnp.maximum(m_near, m_far), m_near)
    near_scale = jnp.exp(m_near - m)
    far_scale = jnp.where(has_far, jnp.exp(m_far - m), 0.0)
    inverse = 1.0 / (near_scale * l_near + far_scale * l_far)
    near_scale = near_scale * inverse
    far_scale = far_scale * inverse
    for h in range(n):
        cols = slice(h * HEAD_DIM, (h + 1) * HEAD_DIM)
        mixed = near_scale[:, h : h + 1] * mixed_ref[:, cols] + far_scale[:, h : h + 1] * o_ref[:, cols].astype(
            jnp.float32
        )
        out_ref[:, cols] = mixed.astype(out_ref.dtype)


def merged_output(block_index, chunk, width, mixed_near, stat_near, o_far, stat_far, previous):
    rows, chunk_width = mixed_near.shape
    step_width = HEADS_PER_STEP * HEAD_DIM
    steps = chunk_width // step_width
    offset = chunk * steps
    part = pl.BlockSpec((rows, step_width), lambda g, b: (0, g))
    whole = pl.BlockSpec((rows, step_width), lambda g, b: (0, g + offset))
    operands = [block_index, mixed_near, stat_near, o_far, stat_far]
    in_specs = [part, stat_spec(rows), part, stat_spec(rows)]
    aliases = {}
    if previous is not None:
        in_specs = in_specs + [pl.BlockSpec(memory_space=pl.ANY)]
        aliases = {len(operands): 0}
        operands = operands + [previous]
    return pl.pallas_call(
        merge_kernel,
        grid_spec=pltpu.PrefetchScalarGridSpec(
            num_scalar_prefetch=1,
            grid=(steps,),
            in_specs=in_specs,
            out_specs=whole,
        ),
        out_shape=jax.ShapeDtypeStruct((rows, width), jnp.bfloat16),
        input_output_aliases=aliases,
    )(*operands)


def per_head(stat):
    steps, rows, _ = stat.shape
    stat = jnp.transpose(stat.reshape(steps, rows, 2, HEADS_PER_STEP), (2, 1, 0, 3))
    return stat[0].reshape(rows, steps * HEADS_PER_STEP), stat[1].reshape(rows, steps * HEADS_PER_STEP)


def log_total(block_index, stat_near, stat_far):
    m_near, l_near = per_head(stat_near)
    m_far, l_far = per_head(stat_far)
    has_far = block_index >= 2
    m = jnp.where(has_far, jnp.maximum(m_near, m_far), m_near)
    total = jnp.exp(m_near - m) * l_near + jnp.where(has_far, jnp.exp(m_far - m), 0.0) * l_far
    return jnp.transpose(m + jnp.log(total))


def shards(att_query, att_key, att_value):
    width = att_query.shape[1]
    chunk_width = width // CHUNKS
    block_index = lax.axis_index("ctx").astype(jnp.int32)
    index_ref = block_index.reshape(1)
    pieces = []
    out = None
    for chunk in range(CHUNKS):
        cols = slice(chunk * chunk_width, (chunk + 1) * chunk_width)
        q, k, v = att_query[:, cols], att_key[:, cols], att_value[:, cols]
        kv_prev = from_behind(jnp.stack([k, v]), "ctx")
        q_next = from_ahead(q, "ctx")
        after = (pieces[-1][1], pieces[-1][3]) if pieces else ()
        o_part, stat_part = partial_attention(q_next, kv_prev, after)
        stat_far = from_behind(stat_part, "ctx")
        if pieces:
            out = merged_output(index_ref, chunk - 1, width, *pieces[-1], out)
        mixed_near, stat_near = near_attention(index_ref, q, k, v, kv_prev, () if out is None else (out,))
        if chunk < CHUNKS - 1:
            o_part, stat_far, mixed_near, stat_near = lax.optimization_barrier((o_part, stat_far, mixed_near, stat_near))
        o_far = from_behind(o_part, "ctx")
        pieces.append((mixed_near, stat_near, o_far, stat_far))
    out = merged_output(index_ref, CHUNKS - 1, width, *pieces[-1], out)
    out, stats = lax.optimization_barrier((out, [(piece[1], piece[3]) for piece in pieces]))
    stat_near = jnp.concatenate([piece[0] for piece in stats], axis=0)
    stat_far = jnp.concatenate([piece[1] for piece in stats], axis=0)
    return out, log_total(block_index, stat_near, stat_far)


def solution(mesh):
    return jax.shard_map(
        shards,
        mesh=mesh,
        in_specs=(P(("dp", "ctx"), None), P(("dp", "ctx"), None), P(("dp", "ctx"), None)),
        out_specs=(P(("dp", "ctx"), None), P(None, ("dp", "ctx"))),
        check_vma=False,
    )
```

```python
import math

import jax
import jax.numpy as jnp
from jax import lax
from jax.experimental import pallas as pl
from jax.experimental.pallas import tpu as pltpu
from jax.sharding import PartitionSpec as P

HEAD_DIM = 128
HEADS_PER_STEP = 8
CHUNKS = 2
SCALE = 1.0 / math.sqrt(HEAD_DIM)
NT_DIMS = (((1,), (1,)), ((), ()))


def from_behind(block, axis):
    devices = range(lax.axis_size(axis))
    route = [(i - 1, i) for i in devices if i - 1 in devices]
    return lax.ppermute(block, axis, route)


def from_ahead(block, axis):
    devices = range(lax.axis_size(axis))
    route = [(i + 1, i) for i in devices if i + 1 in devices]
    return lax.ppermute(block, axis, route)


def weighted_values(weights, values):
    ones = jnp.ones((values.shape[0], HEAD_DIM), values.dtype)
    result = jnp.dot(weights, jnp.concatenate([values, ones], axis=1), preferred_element_type=jnp.float32)
    return result[:, :HEAD_DIM], result[:, HEAD_DIM : HEAD_DIM + 1]


def partial_kernel(q_ref, k_ref, v_ref, *rest):
    o_ref, stat_ref = rest[-2:]
    ones = jnp.ones((q_ref.shape[0], HEAD_DIM), jnp.bfloat16)
    for h in range(HEADS_PER_STEP):
        cols = slice(h * HEAD_DIM, (h + 1) * HEAD_DIM)
        s = lax.dot_general(q_ref[:, cols], k_ref[:, cols], NT_DIMS, preferred_element_type=jnp.float32) * SCALE
        m = jnp.max(s, axis=1, keepdims=True)
        p = jnp.exp(s - m).astype(jnp.bfloat16)
        o_ref[:, cols] = jnp.dot(p, v_ref[:, cols], preferred_element_type=jnp.float32).astype(o_ref.dtype)
        stat_ref[:, h : h + 1] = m
        total = jnp.dot(p, ones, preferred_element_type=jnp.float32)
        stat_ref[:, HEADS_PER_STEP + h : HEADS_PER_STEP + h + 1] = total[:, 0:1]


def near_kernel(block_ref, q_ref, k_ref, v_ref, kp_ref, vp_ref, mixed_ref, stat_ref):
    rows = q_ref.shape[0]
    row_id = lax.broadcasted_iota(jnp.int32, (rows, 2 * rows), 0)
    col_id = lax.broadcasted_iota(jnp.int32, (rows, 2 * rows), 1)
    first_prev = jnp.where(block_ref[0] >= 1, rows, 2 * rows)
    allowed = (col_id <= row_id) | (col_id >= first_prev)
    for h in range(HEADS_PER_STEP):
        cols = slice(h * HEAD_DIM, (h + 1) * HEAD_DIM)
        keys = jnp.concatenate([k_ref[:, cols], kp_ref[:, cols]], axis=0)
        values = jnp.concatenate([v_ref[:, cols], vp_ref[:, cols]], axis=0)
        s = lax.dot_general(q_ref[:, cols], keys, NT_DIMS, preferred_element_type=jnp.float32) * SCALE
        s = jnp.where(allowed, s, -jnp.inf)
        m = jnp.max(s, axis=1, keepdims=True)
        p = jnp.exp(s - m).astype(jnp.bfloat16)
        mixed, total = weighted_values(p, values)
        mixed_ref[:, cols] = mixed
        stat_ref[:, h : h + 1] = m
        stat_ref[:, HEADS_PER_STEP + h : HEADS_PER_STEP + h + 1] = total


def stat_spec(rows):
    return pl.BlockSpec((None, rows, 2 * HEADS_PER_STEP), lambda g, *_: (g, 0, 0))


def partial_attention(q, kv, after=()):
    rows, width = q.shape
    step_width = HEADS_PER_STEP * HEAD_DIM
    steps = width // step_width
    block = pl.BlockSpec((rows, step_width), lambda g: (0, g))
    key_block = pl.BlockSpec((None, rows, step_width), lambda g: (0, 0, g))
    value_block = pl.BlockSpec((None, rows, step_width), lambda g: (1, 0, g))
    return pl.pallas_call(
        partial_kernel,
        grid=(steps,),
        in_specs=[block, key_block, value_block] + [pl.BlockSpec(memory_space=pl.ANY)] * len(after),
        out_specs=[block, stat_spec(rows)],
        out_shape=[
            jax.ShapeDtypeStruct((rows, width), jnp.bfloat16),
            jax.ShapeDtypeStruct((steps, rows, 2 * HEADS_PER_STEP), jnp.float32),
        ],
    )(q, kv, kv, *after)


def near_attention(block_index, q, k, v, kv_prev):
    rows, width = q.shape
    step_width = HEADS_PER_STEP * HEAD_DIM
    steps = width // step_width
    block = pl.BlockSpec((rows, step_width), lambda g, b: (0, g))
    key_block = pl.BlockSpec((None, rows, step_width), lambda g, b: (0, 0, g))
    value_block = pl.BlockSpec((None, rows, step_width), lambda g, b: (1, 0, g))
    return pl.pallas_call(
        near_kernel,
        grid_spec=pltpu.PrefetchScalarGridSpec(
            num_scalar_prefetch=1,
            grid=(steps,),
            in_specs=[block] * 3 + [key_block, value_block],
            out_specs=[block, stat_spec(rows)],
        ),
        out_shape=[
            jax.ShapeDtypeStruct((rows, width), jnp.float32),
            jax.ShapeDtypeStruct((steps, rows, 2 * HEADS_PER_STEP), jnp.float32),
        ],
    )(block_index, q, k, v, kv_prev, kv_prev)


def merge_kernel(block_ref, mixed_ref, near_ref, o_ref, far_ref, *rest):
    out_ref = rest[-1]
    has_far = block_ref[0] >= 2
    n = HEADS_PER_STEP
    near = near_ref[...]
    far = far_ref[...]
    m_near, l_near = near[:, :n], near[:, n:]
    m_far, l_far = far[:, :n], far[:, n:]
    m = jnp.where(has_far, jnp.maximum(m_near, m_far), m_near)
    near_scale = jnp.exp(m_near - m)
    far_scale = jnp.where(has_far, jnp.exp(m_far - m), 0.0)
    inverse = 1.0 / (near_scale * l_near + far_scale * l_far)
    near_scale = near_scale * inverse
    far_scale = far_scale * inverse
    for h in range(n):
        cols = slice(h * HEAD_DIM, (h + 1) * HEAD_DIM)
        mixed = near_scale[:, h : h + 1] * mixed_ref[:, cols] + far_scale[:, h : h + 1] * o_ref[:, cols].astype(
            jnp.float32
        )
        out_ref[:, cols] = mixed.astype(out_ref.dtype)


def merged_output(block_index, chunk, width, mixed_near, stat_near, o_far, stat_far, previous):
    rows, chunk_width = mixed_near.shape
    step_width = HEADS_PER_STEP * HEAD_DIM
    steps = chunk_width // step_width
    offset = chunk * steps
    part = pl.BlockSpec((rows, step_width), lambda g, b: (0, g))
    whole = pl.BlockSpec((rows, step_width), lambda g, b: (0, g + offset))
    operands = [block_index, mixed_near, stat_near, o_far, stat_far]
    in_specs = [part, stat_spec(rows), part, stat_spec(rows)]
    aliases = {}
    if previous is not None:
        in_specs = in_specs + [pl.BlockSpec(memory_space=pl.ANY)]
        aliases = {len(operands): 0}
        operands = operands + [previous]
    return pl.pallas_call(
        merge_kernel,
        grid_spec=pltpu.PrefetchScalarGridSpec(
            num_scalar_prefetch=1,
            grid=(steps,),
            in_specs=in_specs,
            out_specs=whole,
        ),
        out_shape=jax.ShapeDtypeStruct((rows, width), jnp.bfloat16),
        input_output_aliases=aliases,
    )(*operands)


def per_head(stat):
    steps, rows, _ = stat.shape
    stat = jnp.transpose(stat.reshape(steps, rows, 2, HEADS_PER_STEP), (2, 1, 0, 3))
    return stat[0].reshape(rows, steps * HEADS_PER_STEP), stat[1].reshape(rows, steps * HEADS_PER_STEP)


def log_total(block_index, stat_near, stat_far):
    m_near, l_near = per_head(stat_near)
    m_far, l_far = per_head(stat_far)
    has_far = block_index >= 2
    m = jnp.where(has_far, jnp.maximum(m_near, m_far), m_near)
    total = jnp.exp(m_near - m) * l_near + jnp.where(has_far, jnp.exp(m_far - m), 0.0) * l_far
    return jnp.transpose(m + jnp.log(total))


def shards(att_query, att_key, att_value):
    width = att_query.shape[1]
    chunk_width = width // CHUNKS
    block_index = lax.axis_index("ctx").astype(jnp.int32)
    index_ref = block_index.reshape(1)
    pieces = []
    for chunk in range(CHUNKS):
        cols = slice(chunk * chunk_width, (chunk + 1) * chunk_width)
        q, k, v = att_query[:, cols], att_key[:, cols], att_value[:, cols]
        kv_prev = from_behind(jnp.stack([k, v]), "ctx")
        q_next = from_ahead(q, "ctx")
        after = (pieces[-1][1], pieces[-1][3]) if pieces else ()
        o_far, stat_far = from_behind(partial_attention(q_next, kv_prev, after), "ctx")
        mixed_near, stat_near = near_attention(index_ref, q, k, v, kv_prev)
        pieces.append((mixed_near, stat_near, o_far, stat_far))
    out = None
    for chunk in range(CHUNKS):
        out = merged_output(index_ref, chunk, width, *pieces[chunk], out)
    stat_near = jnp.concatenate([piece[1] for piece in pieces], axis=0)
    stat_far = jnp.concatenate([piece[3] for piece in pieces], axis=0)
    return out, log_total(block_index, stat_near, stat_far)


def solution(mesh):
    return jax.shard_map(
        shards,
        mesh=mesh,
        in_specs=(P(("dp", "ctx"), None), P(("dp", "ctx"), None), P(("dp", "ctx"), None)),
        out_specs=(P(("dp", "ctx"), None), P(None, ("dp", "ctx"))),
        check_vma=False,
    )
```

```python
import math

import jax
import jax.numpy as jnp
from jax import lax
from jax.experimental import pallas as pl
from jax.experimental.pallas import tpu as pltpu
from jax.sharding import PartitionSpec as P

HEAD_DIM = 128
HEADS_PER_STEP = 8
CHUNKS = 2
SCALE = 1.0 / math.sqrt(HEAD_DIM)
NT_DIMS = (((1,), (1,)), ((), ()))


def from_behind(block, axis):
    devices = range(lax.axis_size(axis))
    route = [(i - 1, i) for i in devices if i - 1 in devices]
    return lax.ppermute(block, axis, route)


def from_ahead(block, axis):
    devices = range(lax.axis_size(axis))
    route = [(i + 1, i) for i in devices if i + 1 in devices]
    return lax.ppermute(block, axis, route)


def weighted_values(weights, values):
    ones = jnp.ones((values.shape[0], HEAD_DIM), values.dtype)
    result = jnp.dot(weights, jnp.concatenate([values, ones], axis=1), preferred_element_type=jnp.float32)
    return result[:, :HEAD_DIM], result[:, HEAD_DIM : HEAD_DIM + 1]


def partial_kernel(q_ref, k_ref, v_ref, *rest):
    o_ref, stat_ref = rest[-2:]
    ones = jnp.ones((q_ref.shape[0], HEAD_DIM), jnp.bfloat16)
    for h in range(HEADS_PER_STEP):
        cols = slice(h * HEAD_DIM, (h + 1) * HEAD_DIM)
        s = lax.dot_general(q_ref[:, cols], k_ref[:, cols], NT_DIMS, preferred_element_type=jnp.float32) * SCALE
        m = jnp.max(s, axis=1, keepdims=True)
        p = jnp.exp(s - m).astype(jnp.bfloat16)
        o_ref[:, cols] = jnp.dot(p, v_ref[:, cols], preferred_element_type=jnp.float32).astype(o_ref.dtype)
        stat_ref[:, h : h + 1] = m
        total = jnp.dot(p, ones, preferred_element_type=jnp.float32)
        stat_ref[:, HEADS_PER_STEP + h : HEADS_PER_STEP + h + 1] = total[:, 0:1]


def near_kernel(block_ref, q_ref, k_ref, v_ref, kp_ref, vp_ref, mixed_ref, stat_ref):
    rows = q_ref.shape[0]
    row_id = lax.broadcasted_iota(jnp.int32, (rows, 2 * rows), 0)
    col_id = lax.broadcasted_iota(jnp.int32, (rows, 2 * rows), 1)
    first_prev = jnp.where(block_ref[0] >= 1, rows, 2 * rows)
    allowed = (col_id <= row_id) | (col_id >= first_prev)
    for h in range(HEADS_PER_STEP):
        cols = slice(h * HEAD_DIM, (h + 1) * HEAD_DIM)
        keys = jnp.concatenate([k_ref[:, cols], kp_ref[:, cols]], axis=0)
        values = jnp.concatenate([v_ref[:, cols], vp_ref[:, cols]], axis=0)
        s = lax.dot_general(q_ref[:, cols], keys, NT_DIMS, preferred_element_type=jnp.float32) * SCALE
        s = jnp.where(allowed, s, -jnp.inf)
        m = jnp.max(s, axis=1, keepdims=True)
        p = jnp.exp(s - m).astype(jnp.bfloat16)
        mixed, total = weighted_values(p, values)
        mixed_ref[:, cols] = mixed
        stat_ref[:, h : h + 1] = m
        stat_ref[:, HEADS_PER_STEP + h : HEADS_PER_STEP + h + 1] = total


def stat_spec(rows):
    return pl.BlockSpec((None, rows, 2 * HEADS_PER_STEP), lambda g, *_: (g, 0, 0))


def partial_attention(q, kv, after=()):
    rows, width = q.shape
    step_width = HEADS_PER_STEP * HEAD_DIM
    steps = width // step_width
    block = pl.BlockSpec((rows, step_width), lambda g: (0, g))
    key_block = pl.BlockSpec((None, rows, step_width), lambda g: (0, 0, g))
    value_block = pl.BlockSpec((None, rows, step_width), lambda g: (1, 0, g))
    return pl.pallas_call(
        partial_kernel,
        grid=(steps,),
        in_specs=[block, key_block, value_block] + [pl.BlockSpec(memory_space=pl.ANY)] * len(after),
        out_specs=[block, stat_spec(rows)],
        out_shape=[
            jax.ShapeDtypeStruct((rows, width), jnp.bfloat16),
            jax.ShapeDtypeStruct((steps, rows, 2 * HEADS_PER_STEP), jnp.float32),
        ],
    )(q, kv, kv, *after)


def near_attention(block_index, chunk, q, k, v, kv_prev):
    rows, width = q.shape
    step_width = HEADS_PER_STEP * HEAD_DIM
    steps = kv_prev.shape[2] // step_width
    offset = chunk * steps
    whole = pl.BlockSpec((rows, step_width), lambda g, b: (0, g + offset))
    part = pl.BlockSpec((rows, step_width), lambda g, b: (0, g))
    key_block = pl.BlockSpec((None, rows, step_width), lambda g, b: (0, 0, g))
    value_block = pl.BlockSpec((None, rows, step_width), lambda g, b: (1, 0, g))
    return pl.pallas_call(
        near_kernel,
        grid_spec=pltpu.PrefetchScalarGridSpec(
            num_scalar_prefetch=1,
            grid=(steps,),
            in_specs=[whole] * 3 + [key_block, value_block],
            out_specs=[part, stat_spec(rows)],
        ),
        out_shape=[
            jax.ShapeDtypeStruct((rows, kv_prev.shape[2]), jnp.float32),
            jax.ShapeDtypeStruct((steps, rows, 2 * HEADS_PER_STEP), jnp.float32),
        ],
    )(block_index, q, k, v, kv_prev, kv_prev)


def merge_kernel(block_ref, mixed_ref, near_ref, o_ref, far_ref, *rest):
    out_ref = rest[-1]
    has_far = block_ref[0] >= 2
    n = HEADS_PER_STEP
    near = near_ref[...]
    far = far_ref[...]
    m_near, l_near = near[:, :n], near[:, n:]
    m_far, l_far = far[:, :n], far[:, n:]
    m = jnp.where(has_far, jnp.maximum(m_near, m_far), m_near)
    near_scale = jnp.exp(m_near - m)
    far_scale = jnp.where(has_far, jnp.exp(m_far - m), 0.0)
    inverse = 1.0 / (near_scale * l_near + far_scale * l_far)
    near_scale = near_scale * inverse
    far_scale = far_scale * inverse
    for h in range(n):
        cols = slice(h * HEAD_DIM, (h + 1) * HEAD_DIM)
        mixed = near_scale[:, h : h + 1] * mixed_ref[:, cols] + far_scale[:, h : h + 1] * o_ref[:, cols].astype(
            jnp.float32
        )
        out_ref[:, cols] = mixed.astype(out_ref.dtype)


def merged_output(block_index, chunk, width, mixed_near, stat_near, o_far, stat_far, previous):
    rows, chunk_width = mixed_near.shape
    step_width = HEADS_PER_STEP * HEAD_DIM
    steps = chunk_width // step_width
    offset = chunk * steps
    part = pl.BlockSpec((rows, step_width), lambda g, b: (0, g))
    whole = pl.BlockSpec((rows, step_width), lambda g, b: (0, g + offset))
    operands = [block_index, mixed_near, stat_near, o_far, stat_far]
    in_specs = [part, stat_spec(rows), part, stat_spec(rows)]
    aliases = {}
    if previous is not None:
        in_specs = in_specs + [pl.BlockSpec(memory_space=pl.ANY)]
        aliases = {len(operands): 0}
        operands = operands + [previous]
    return pl.pallas_call(
        merge_kernel,
        grid_spec=pltpu.PrefetchScalarGridSpec(
            num_scalar_prefetch=1,
            grid=(steps,),
            in_specs=in_specs,
            out_specs=whole,
        ),
        out_shape=jax.ShapeDtypeStruct((rows, width), jnp.bfloat16),
        input_output_aliases=aliases,
    )(*operands)


def per_head(stat):
    steps, rows, _ = stat.shape
    stat = jnp.transpose(stat.reshape(steps, rows, 2, HEADS_PER_STEP), (2, 1, 0, 3))
    return stat[0].reshape(rows, steps * HEADS_PER_STEP), stat[1].reshape(rows, steps * HEADS_PER_STEP)


def log_total(block_index, stat_near, stat_far):
    m_near, l_near = per_head(stat_near)
    m_far, l_far = per_head(stat_far)
    has_far = block_index >= 2
    m = jnp.where(has_far, jnp.maximum(m_near, m_far), m_near)
    total = jnp.exp(m_near - m) * l_near + jnp.where(has_far, jnp.exp(m_far - m), 0.0) * l_far
    return jnp.transpose(m + jnp.log(total))


def shards(att_query, att_key, att_value):
    width = att_query.shape[1]
    chunk_width = width // CHUNKS
    block_index = lax.axis_index("ctx").astype(jnp.int32)
    index_ref = block_index.reshape(1)
    pieces = []
    for chunk in range(CHUNKS):
        cols = slice(chunk * chunk_width, (chunk + 1) * chunk_width)
        kv_prev = from_behind(jnp.stack([att_key[:, cols], att_value[:, cols]]), "ctx")
        q_next = from_ahead(att_query[:, cols], "ctx")
        after = (pieces[-1][1], pieces[-1][3]) if pieces else ()
        o_far, stat_far = from_behind(partial_attention(q_next, kv_prev, after), "ctx")
        mixed_near, stat_near = near_attention(index_ref, chunk, att_query, att_key, att_value, kv_prev)
        pieces.append((mixed_near, stat_near, o_far, stat_far))
    out = None
    for chunk in range(CHUNKS):
        out = merged_output(index_ref, chunk, width, *pieces[chunk], out)
    stat_near = jnp.concatenate([piece[1] for piece in pieces], axis=0)
    stat_far = jnp.concatenate([piece[3] for piece in pieces], axis=0)
    return out, log_total(block_index, stat_near, stat_far)


def solution(mesh):
    return jax.shard_map(
        shards,
        mesh=mesh,
        in_specs=(P(("dp", "ctx"), None), P(("dp", "ctx"), None), P(("dp", "ctx"), None)),
        out_specs=(P(("dp", "ctx"), None), P(None, ("dp", "ctx"))),
        check_vma=False,
    )
```

```python
import math

import jax
import jax.numpy as jnp
from jax import lax
from jax.experimental import pallas as pl
from jax.experimental.pallas import tpu as pltpu
from jax.sharding import PartitionSpec as P

HEAD_DIM = 128
HEADS_PER_STEP = 8
CHUNKS = 2
SCALE = 1.0 / math.sqrt(HEAD_DIM)
NT_DIMS = (((1,), (1,)), ((), ()))


def from_behind(block, axis):
    devices = range(lax.axis_size(axis))
    route = [(i - 1, i) for i in devices if i - 1 in devices]
    return lax.ppermute(block, axis, route)


def from_ahead(block, axis):
    devices = range(lax.axis_size(axis))
    route = [(i + 1, i) for i in devices if i + 1 in devices]
    return lax.ppermute(block, axis, route)


def weighted_values(weights, values):
    ones = jnp.ones((values.shape[0], HEAD_DIM), values.dtype)
    result = jnp.dot(weights, jnp.concatenate([values, ones], axis=1), preferred_element_type=jnp.float32)
    return result[:, :HEAD_DIM], result[:, HEAD_DIM : HEAD_DIM + 1]


def partial_kernel(q_ref, k_ref, v_ref, *rest):
    o_ref, stat_ref = rest[-2:]
    ones = jnp.ones((q_ref.shape[0], HEAD_DIM), jnp.bfloat16)
    for h in range(HEADS_PER_STEP):
        cols = slice(h * HEAD_DIM, (h + 1) * HEAD_DIM)
        s = lax.dot_general(q_ref[:, cols], k_ref[:, cols], NT_DIMS, preferred_element_type=jnp.float32) * SCALE
        m = jnp.max(s, axis=1, keepdims=True)
        p = jnp.exp(s - m).astype(jnp.bfloat16)
        o_ref[:, cols] = jnp.dot(p, v_ref[:, cols], preferred_element_type=jnp.float32).astype(o_ref.dtype)
        stat_ref[:, h : h + 1] = m
        total = jnp.dot(p, ones, preferred_element_type=jnp.float32)
        stat_ref[:, HEADS_PER_STEP + h : HEADS_PER_STEP + h + 1] = total[:, 0:1]


def near_kernel(block_ref, q_ref, k_ref, v_ref, kp_ref, vp_ref, mixed_ref, stat_ref):
    rows = q_ref.shape[0]
    row_id = lax.broadcasted_iota(jnp.int32, (rows, 2 * rows), 0)
    col_id = lax.broadcasted_iota(jnp.int32, (rows, 2 * rows), 1)
    first_prev = jnp.where(block_ref[0] >= 1, rows, 2 * rows)
    allowed = (col_id <= row_id) | (col_id >= first_prev)
    for h in range(HEADS_PER_STEP):
        cols = slice(h * HEAD_DIM, (h + 1) * HEAD_DIM)
        keys = jnp.concatenate([k_ref[:, cols], kp_ref[:, cols]], axis=0)
        values = jnp.concatenate([v_ref[:, cols], vp_ref[:, cols]], axis=0)
        s = lax.dot_general(q_ref[:, cols], keys, NT_DIMS, preferred_element_type=jnp.float32) * SCALE
        s = jnp.where(allowed, s, -jnp.inf)
        m = jnp.max(s, axis=1, keepdims=True)
        p = jnp.exp(s - m).astype(jnp.bfloat16)
        mixed, total = weighted_values(p, values)
        mixed_ref[:, cols] = mixed
        stat_ref[:, h : h + 1] = m
        stat_ref[:, HEADS_PER_STEP + h : HEADS_PER_STEP + h + 1] = total


def stat_spec(rows):
    return pl.BlockSpec((None, rows, 2 * HEADS_PER_STEP), lambda g, *_: (g, 0, 0))


def partial_attention(q, kv, after=()):
    rows, width = q.shape
    step_width = HEADS_PER_STEP * HEAD_DIM
    steps = width // step_width
    block = pl.BlockSpec((rows, step_width), lambda g: (0, g))
    key_block = pl.BlockSpec((None, rows, step_width), lambda g: (0, 0, g))
    value_block = pl.BlockSpec((None, rows, step_width), lambda g: (1, 0, g))
    return pl.pallas_call(
        partial_kernel,
        grid=(steps,),
        in_specs=[block, key_block, value_block] + [pl.BlockSpec(memory_space=pl.ANY)] * len(after),
        out_specs=[block, stat_spec(rows)],
        out_shape=[
            jax.ShapeDtypeStruct((rows, width), jnp.bfloat16),
            jax.ShapeDtypeStruct((steps, rows, 2 * HEADS_PER_STEP), jnp.float32),
        ],
    )(q, kv, kv, *after)


def near_attention(block_index, chunk, q, k, v, kv_prev):
    rows, width = q.shape
    step_width = HEADS_PER_STEP * HEAD_DIM
    steps = kv_prev.shape[2] // step_width
    offset = chunk * steps
    whole = pl.BlockSpec((rows, step_width), lambda g, b: (0, g + offset))
    part = pl.BlockSpec((rows, step_width), lambda g, b: (0, g))
    key_block = pl.BlockSpec((None, rows, step_width), lambda g, b: (0, 0, g))
    value_block = pl.BlockSpec((None, rows, step_width), lambda g, b: (1, 0, g))
    return pl.pallas_call(
        near_kernel,
        grid_spec=pltpu.PrefetchScalarGridSpec(
            num_scalar_prefetch=1,
            grid=(steps,),
            in_specs=[whole] * 3 + [key_block, value_block],
            out_specs=[part, stat_spec(rows)],
        ),
        out_shape=[
            jax.ShapeDtypeStruct((rows, kv_prev.shape[2]), jnp.float32),
            jax.ShapeDtypeStruct((steps, rows, 2 * HEADS_PER_STEP), jnp.float32),
        ],
    )(block_index, q, k, v, kv_prev, kv_prev)


def merge_kernel(block_ref, mixed_ref, near_ref, o_ref, far_ref, *rest):
    out_ref = rest[-1]
    has_far = block_ref[0] >= 2
    n = HEADS_PER_STEP
    near = near_ref[...]
    far = far_ref[...]
    m_near, l_near = near[:, :n], near[:, n:]
    m_far, l_far = far[:, :n], far[:, n:]
    m = jnp.where(has_far, jnp.maximum(m_near, m_far), m_near)
    near_scale = jnp.exp(m_near - m)
    far_scale = jnp.where(has_far, jnp.exp(m_far - m), 0.0)
    inverse = 1.0 / (near_scale * l_near + far_scale * l_far)
    near_scale = near_scale * inverse
    far_scale = far_scale * inverse
    for h in range(n):
        cols = slice(h * HEAD_DIM, (h + 1) * HEAD_DIM)
        mixed = near_scale[:, h : h + 1] * mixed_ref[:, cols] + far_scale[:, h : h + 1] * o_ref[:, cols].astype(
            jnp.float32
        )
        out_ref[:, cols] = mixed.astype(out_ref.dtype)


def merged_output(block_index, chunk, width, mixed_near, stat_near, o_far, stat_far, previous):
    rows, chunk_width = mixed_near.shape
    step_width = HEADS_PER_STEP * HEAD_DIM
    steps = chunk_width // step_width
    offset = chunk * steps
    part = pl.BlockSpec((rows, step_width), lambda g, b: (0, g))
    whole = pl.BlockSpec((rows, step_width), lambda g, b: (0, g + offset))
    operands = [block_index, mixed_near, stat_near, o_far, stat_far]
    in_specs = [part, stat_spec(rows), part, stat_spec(rows)]
    aliases = {}
    if previous is not None:
        in_specs = in_specs + [pl.BlockSpec(memory_space=pl.ANY)]
        aliases = {len(operands): 0}
        operands = operands + [previous]
    return pl.pallas_call(
        merge_kernel,
        grid_spec=pltpu.PrefetchScalarGridSpec(
            num_scalar_prefetch=1,
            grid=(steps,),
            in_specs=in_specs,
            out_specs=whole,
        ),
        out_shape=jax.ShapeDtypeStruct((rows, width), jnp.bfloat16),
        input_output_aliases=aliases,
    )(*operands)


def per_head(stat):
    steps, rows, _ = stat.shape
    stat = jnp.transpose(stat.reshape(steps, rows, 2, HEADS_PER_STEP), (2, 1, 0, 3))
    return stat[0].reshape(rows, steps * HEADS_PER_STEP), stat[1].reshape(rows, steps * HEADS_PER_STEP)


def log_total(block_index, stat_near, stat_far):
    m_near, l_near = per_head(stat_near)
    m_far, l_far = per_head(stat_far)
    has_far = block_index >= 2
    m = jnp.where(has_far, jnp.maximum(m_near, m_far), m_near)
    total = jnp.exp(m_near - m) * l_near + jnp.where(has_far, jnp.exp(m_far - m), 0.0) * l_far
    return jnp.transpose(m + jnp.log(total))


def shards(att_query, att_key, att_value):
    width = att_query.shape[1]
    chunk_width = width // CHUNKS
    block_index = lax.axis_index("ctx").astype(jnp.int32)
    index_ref = block_index.reshape(1)
    pieces = []
    for chunk in range(CHUNKS):
        cols = slice(chunk * chunk_width, (chunk + 1) * chunk_width)
        kv_prev = from_behind(jnp.stack([att_key[:, cols], att_value[:, cols]]), "ctx")
        q_next = from_ahead(att_query[:, cols], "ctx")
        after = (pieces[-1][1], pieces[-1][3]) if pieces else ()
        o_far, stat_far = from_behind(partial_attention(q_next, kv_prev, after), "ctx")
        mixed_near, stat_near = near_attention(index_ref, chunk, att_query, att_key, att_value, kv_prev)
        pieces.append((mixed_near, stat_near, o_far, stat_far))
    out = None
    for chunk in range(CHUNKS):
        out = merged_output(index_ref, chunk, width, *pieces[chunk], out)
    out, stats = lax.optimization_barrier((out, [(piece[1], piece[3]) for piece in pieces]))
    stat_near = jnp.concatenate([piece[0] for piece in stats], axis=0)
    stat_far = jnp.concatenate([piece[1] for piece in stats], axis=0)
    return out, log_total(block_index, stat_near, stat_far)


def solution(mesh):
    return jax.shard_map(
        shards,
        mesh=mesh,
        in_specs=(P(("dp", "ctx"), None), P(("dp", "ctx"), None), P(("dp", "ctx"), None)),
        out_specs=(P(("dp", "ctx"), None), P(None, ("dp", "ctx"))),
        check_vma=False,
    )
```

```python
import math

import jax
import jax.numpy as jnp
from jax import lax
from jax.experimental import pallas as pl
from jax.experimental.pallas import tpu as pltpu
from jax.sharding import PartitionSpec as P

HEAD_DIM = 128
HEADS_PER_STEP = 16
CHUNKS = 2
SCALE = 1.0 / math.sqrt(HEAD_DIM)
NT_DIMS = (((1,), (1,)), ((), ()))


def from_behind(block, axis):
    devices = range(lax.axis_size(axis))
    route = [(i - 1, i) for i in devices if i - 1 in devices]
    return lax.ppermute(block, axis, route)


def from_ahead(block, axis):
    devices = range(lax.axis_size(axis))
    route = [(i + 1, i) for i in devices if i + 1 in devices]
    return lax.ppermute(block, axis, route)


def weighted_values(weights, values):
    ones = jnp.ones((values.shape[0], HEAD_DIM), values.dtype)
    result = jnp.dot(weights, jnp.concatenate([values, ones], axis=1), preferred_element_type=jnp.float32)
    return result[:, :HEAD_DIM], result[:, HEAD_DIM : HEAD_DIM + 1]


def partial_kernel(q_ref, k_ref, v_ref, *rest):
    o_ref, stat_ref = rest[-2:]
    ones = jnp.ones((q_ref.shape[0], HEAD_DIM), jnp.bfloat16)
    for h in range(HEADS_PER_STEP):
        cols = slice(h * HEAD_DIM, (h + 1) * HEAD_DIM)
        s = lax.dot_general(q_ref[:, cols], k_ref[:, cols], NT_DIMS, preferred_element_type=jnp.float32) * SCALE
        m = jnp.max(s, axis=1, keepdims=True)
        p = jnp.exp(s - m).astype(jnp.bfloat16)
        o_ref[:, cols] = jnp.dot(p, v_ref[:, cols], preferred_element_type=jnp.float32).astype(o_ref.dtype)
        stat_ref[:, h : h + 1] = m
        total = jnp.dot(p, ones, preferred_element_type=jnp.float32)
        stat_ref[:, HEADS_PER_STEP + h : HEADS_PER_STEP + h + 1] = total[:, 0:1]


def near_kernel(block_ref, q_ref, k_ref, v_ref, kp_ref, vp_ref, mixed_ref, stat_ref):
    rows = q_ref.shape[0]
    row_id = lax.broadcasted_iota(jnp.int32, (rows, 2 * rows), 0)
    col_id = lax.broadcasted_iota(jnp.int32, (rows, 2 * rows), 1)
    first_prev = jnp.where(block_ref[0] >= 1, rows, 2 * rows)
    allowed = (col_id <= row_id) | (col_id >= first_prev)
    for h in range(HEADS_PER_STEP):
        cols = slice(h * HEAD_DIM, (h + 1) * HEAD_DIM)
        keys = jnp.concatenate([k_ref[:, cols], kp_ref[:, cols]], axis=0)
        values = jnp.concatenate([v_ref[:, cols], vp_ref[:, cols]], axis=0)
        s = lax.dot_general(q_ref[:, cols], keys, NT_DIMS, preferred_element_type=jnp.float32) * SCALE
        s = jnp.where(allowed, s, -jnp.inf)
        m = jnp.max(s, axis=1, keepdims=True)
        p = jnp.exp(s - m).astype(jnp.bfloat16)
        mixed, total = weighted_values(p, values)
        mixed_ref[:, cols] = mixed
        stat_ref[:, h : h + 1] = m
        stat_ref[:, HEADS_PER_STEP + h : HEADS_PER_STEP + h + 1] = total


def stat_spec(rows):
    return pl.BlockSpec((None, rows, 2 * HEADS_PER_STEP), lambda g, *_: (g, 0, 0))


def partial_attention(q, kv, after=()):
    rows, width = q.shape
    step_width = HEADS_PER_STEP * HEAD_DIM
    steps = width // step_width
    block = pl.BlockSpec((rows, step_width), lambda g: (0, g))
    key_block = pl.BlockSpec((None, rows, step_width), lambda g: (0, 0, g))
    value_block = pl.BlockSpec((None, rows, step_width), lambda g: (1, 0, g))
    return pl.pallas_call(
        partial_kernel,
        grid=(steps,),
        in_specs=[block, key_block, value_block] + [pl.BlockSpec(memory_space=pl.ANY)] * len(after),
        out_specs=[block, stat_spec(rows)],
        out_shape=[
            jax.ShapeDtypeStruct((rows, width), jnp.bfloat16),
            jax.ShapeDtypeStruct((steps, rows, 2 * HEADS_PER_STEP), jnp.float32),
        ],
    )(q, kv, kv, *after)


def near_attention(block_index, chunk, q, k, v, kv_prev):
    rows, width = q.shape
    step_width = HEADS_PER_STEP * HEAD_DIM
    steps = kv_prev.shape[2] // step_width
    offset = chunk * steps
    whole = pl.BlockSpec((rows, step_width), lambda g, b: (0, g + offset))
    part = pl.BlockSpec((rows, step_width), lambda g, b: (0, g))
    key_block = pl.BlockSpec((None, rows, step_width), lambda g, b: (0, 0, g))
    value_block = pl.BlockSpec((None, rows, step_width), lambda g, b: (1, 0, g))
    return pl.pallas_call(
        near_kernel,
        grid_spec=pltpu.PrefetchScalarGridSpec(
            num_scalar_prefetch=1,
            grid=(steps,),
            in_specs=[whole] * 3 + [key_block, value_block],
            out_specs=[part, stat_spec(rows)],
        ),
        out_shape=[
            jax.ShapeDtypeStruct((rows, kv_prev.shape[2]), jnp.float32),
            jax.ShapeDtypeStruct((steps, rows, 2 * HEADS_PER_STEP), jnp.float32),
        ],
    )(block_index, q, k, v, kv_prev, kv_prev)


def merge_kernel(block_ref, mixed_ref, near_ref, o_ref, far_ref, *rest):
    out_ref = rest[-1]
    has_far = block_ref[0] >= 2
    n = HEADS_PER_STEP
    near = near_ref[...]
    far = far_ref[...]
    m_near, l_near = near[:, :n], near[:, n:]
    m_far, l_far = far[:, :n], far[:, n:]
    m = jnp.where(has_far, jnp.maximum(m_near, m_far), m_near)
    near_scale = jnp.exp(m_near - m)
    far_scale = jnp.where(has_far, jnp.exp(m_far - m), 0.0)
    inverse = 1.0 / (near_scale * l_near + far_scale * l_far)
    near_scale = near_scale * inverse
    far_scale = far_scale * inverse
    for h in range(n):
        cols = slice(h * HEAD_DIM, (h + 1) * HEAD_DIM)
        mixed = near_scale[:, h : h + 1] * mixed_ref[:, cols] + far_scale[:, h : h + 1] * o_ref[:, cols].astype(
            jnp.float32
        )
        out_ref[:, cols] = mixed.astype(out_ref.dtype)


def merged_output(block_index, chunk, width, mixed_near, stat_near, o_far, stat_far, previous):
    rows, chunk_width = mixed_near.shape
    step_width = HEADS_PER_STEP * HEAD_DIM
    steps = chunk_width // step_width
    offset = chunk * steps
    part = pl.BlockSpec((rows, step_width), lambda g, b: (0, g))
    whole = pl.BlockSpec((rows, step_width), lambda g, b: (0, g + offset))
    operands = [block_index, mixed_near, stat_near, o_far, stat_far]
    in_specs = [part, stat_spec(rows), part, stat_spec(rows)]
    aliases = {}
    if previous is not None:
        in_specs = in_specs + [pl.BlockSpec(memory_space=pl.ANY)]
        aliases = {len(operands): 0}
        operands = operands + [previous]
    return pl.pallas_call(
        merge_kernel,
        grid_spec=pltpu.PrefetchScalarGridSpec(
            num_scalar_prefetch=1,
            grid=(steps,),
            in_specs=in_specs,
            out_specs=whole,
        ),
        out_shape=jax.ShapeDtypeStruct((rows, width), jnp.bfloat16),
        input_output_aliases=aliases,
    )(*operands)


def per_head(stat):
    steps, rows, _ = stat.shape
    stat = jnp.transpose(stat.reshape(steps, rows, 2, HEADS_PER_STEP), (2, 1, 0, 3))
    return stat[0].reshape(rows, steps * HEADS_PER_STEP), stat[1].reshape(rows, steps * HEADS_PER_STEP)


def log_total(block_index, stat_near, stat_far):
    m_near, l_near = per_head(stat_near)
    m_far, l_far = per_head(stat_far)
    has_far = block_index >= 2
    m = jnp.where(has_far, jnp.maximum(m_near, m_far), m_near)
    total = jnp.exp(m_near - m) * l_near + jnp.where(has_far, jnp.exp(m_far - m), 0.0) * l_far
    return jnp.transpose(m + jnp.log(total))


def shards(att_query, att_key, att_value):
    width = att_query.shape[1]
    chunk_width = width // CHUNKS
    block_index = lax.axis_index("ctx").astype(jnp.int32)
    index_ref = block_index.reshape(1)
    pieces = []
    for chunk in range(CHUNKS):
        cols = slice(chunk * chunk_width, (chunk + 1) * chunk_width)
        kv_prev = from_behind(jnp.stack([att_key[:, cols], att_value[:, cols]]), "ctx")
        q_next = from_ahead(att_query[:, cols], "ctx")
        after = (pieces[-1][1], pieces[-1][3]) if pieces else ()
        o_far, stat_far = from_behind(partial_attention(q_next, kv_prev, after), "ctx")
        mixed_near, stat_near = near_attention(index_ref, chunk, att_query, att_key, att_value, kv_prev)
        pieces.append((mixed_near, stat_near, o_far, stat_far))
    out = None
    for chunk in range(CHUNKS):
        out = merged_output(index_ref, chunk, width, *pieces[chunk], out)
    out, stats = lax.optimization_barrier((out, [(piece[1], piece[3]) for piece in pieces]))
    stat_near = jnp.concatenate([piece[0] for piece in stats], axis=0)
    stat_far = jnp.concatenate([piece[1] for piece in stats], axis=0)
    return out, log_total(block_index, stat_near, stat_far)


def solution(mesh):
    return jax.shard_map(
        shards,
        mesh=mesh,
        in_specs=(P(("dp", "ctx"), None), P(("dp", "ctx"), None), P(("dp", "ctx"), None)),
        out_specs=(P(("dp", "ctx"), None), P(None, ("dp", "ctx"))),
        check_vma=False,
    )
```

```python
import math

import jax
import jax.numpy as jnp
from jax import lax
from jax.experimental import pallas as pl
from jax.experimental.pallas import tpu as pltpu
from jax.sharding import PartitionSpec as P

HEAD_DIM = 128
HEADS_PER_STEP = 16
CHUNKS = 2
SCALE = 1.0 / math.sqrt(HEAD_DIM)
NT_DIMS = (((1,), (1,)), ((), ()))


def from_behind(block, axis):
    devices = range(lax.axis_size(axis))
    route = [(i - 1, i) for i in devices if i - 1 in devices]
    return lax.ppermute(block, axis, route)


def from_ahead(block, axis):
    devices = range(lax.axis_size(axis))
    route = [(i + 1, i) for i in devices if i + 1 in devices]
    return lax.ppermute(block, axis, route)


def weighted_values(weights, values):
    ones = jnp.ones((values.shape[0], HEAD_DIM), values.dtype)
    result = jnp.dot(weights, jnp.concatenate([values, ones], axis=1), preferred_element_type=jnp.float32)
    return result[:, :HEAD_DIM], result[:, HEAD_DIM : HEAD_DIM + 1]


def partial_kernel(q_ref, k_ref, v_ref, *rest):
    o_ref, stat_ref = rest[-2:]
    ones = jnp.ones((q_ref.shape[0], HEAD_DIM), jnp.bfloat16)
    for h in range(HEADS_PER_STEP):
        cols = slice(h * HEAD_DIM, (h + 1) * HEAD_DIM)
        s = lax.dot_general(q_ref[:, cols], k_ref[:, cols], NT_DIMS, preferred_element_type=jnp.float32) * SCALE
        m = jnp.max(s, axis=1, keepdims=True)
        p = jnp.exp(s - m).astype(jnp.bfloat16)
        o_ref[:, cols] = jnp.dot(p, v_ref[:, cols], preferred_element_type=jnp.float32).astype(o_ref.dtype)
        stat_ref[:, h : h + 1] = m
        total = jnp.dot(p, ones, preferred_element_type=jnp.float32)
        stat_ref[:, HEADS_PER_STEP + h : HEADS_PER_STEP + h + 1] = total[:, 0:1]


def near_kernel(block_ref, q_ref, k_ref, v_ref, kp_ref, vp_ref, mixed_ref, stat_ref):
    rows = q_ref.shape[0]
    row_id = lax.broadcasted_iota(jnp.int32, (rows, 2 * rows), 0)
    col_id = lax.broadcasted_iota(jnp.int32, (rows, 2 * rows), 1)
    first_prev = jnp.where(block_ref[0] >= 1, rows, 2 * rows)
    allowed = (col_id <= row_id) | (col_id >= first_prev)
    for h in range(HEADS_PER_STEP):
        cols = slice(h * HEAD_DIM, (h + 1) * HEAD_DIM)
        keys = jnp.concatenate([k_ref[:, cols], kp_ref[:, cols]], axis=0)
        values = jnp.concatenate([v_ref[:, cols], vp_ref[:, cols]], axis=0)
        s = lax.dot_general(q_ref[:, cols], keys, NT_DIMS, preferred_element_type=jnp.float32) * SCALE
        s = jnp.where(allowed, s, -jnp.inf)
        m = jnp.max(s, axis=1, keepdims=True)
        p = jnp.exp(s - m).astype(jnp.bfloat16)
        mixed, total = weighted_values(p, values)
        mixed_ref[:, cols] = mixed
        stat_ref[:, h : h + 1] = m
        stat_ref[:, HEADS_PER_STEP + h : HEADS_PER_STEP + h + 1] = total


def stat_spec(rows):
    return pl.BlockSpec((None, rows, 2 * HEADS_PER_STEP), lambda g, *_: (g, 0, 0))


def partial_attention(q, kv, after=()):
    rows, width = q.shape
    step_width = HEADS_PER_STEP * HEAD_DIM
    steps = width // step_width
    block = pl.BlockSpec((rows, step_width), lambda g: (0, g))
    key_block = pl.BlockSpec((None, rows, step_width), lambda g: (0, 0, g))
    value_block = pl.BlockSpec((None, rows, step_width), lambda g: (1, 0, g))
    return pl.pallas_call(
        partial_kernel,
        grid=(steps,),
        in_specs=[block, key_block, value_block] + [pl.BlockSpec(memory_space=pl.ANY)] * len(after),
        out_specs=[block, stat_spec(rows)],
        out_shape=[
            jax.ShapeDtypeStruct((rows, width), jnp.bfloat16),
            jax.ShapeDtypeStruct((steps, rows, 2 * HEADS_PER_STEP), jnp.float32),
        ],
    )(q, kv, kv, *after)


def near_attention(block_index, chunk, q, k, v, kv_prev):
    rows, width = q.shape
    step_width = HEADS_PER_STEP * HEAD_DIM
    steps = kv_prev.shape[2] // step_width
    offset = chunk * steps
    whole = pl.BlockSpec((rows, step_width), lambda g, b: (0, g + offset))
    part = pl.BlockSpec((rows, step_width), lambda g, b: (0, g))
    key_block = pl.BlockSpec((None, rows, step_width), lambda g, b: (0, 0, g))
    value_block = pl.BlockSpec((None, rows, step_width), lambda g, b: (1, 0, g))
    return pl.pallas_call(
        near_kernel,
        grid_spec=pltpu.PrefetchScalarGridSpec(
            num_scalar_prefetch=1,
            grid=(steps,),
            in_specs=[whole] * 3 + [key_block, value_block],
            out_specs=[part, stat_spec(rows)],
        ),
        out_shape=[
            jax.ShapeDtypeStruct((rows, kv_prev.shape[2]), jnp.float32),
            jax.ShapeDtypeStruct((steps, rows, 2 * HEADS_PER_STEP), jnp.float32),
        ],
    )(block_index, q, k, v, kv_prev, kv_prev)


def merge_kernel(block_ref, mixed_ref, near_ref, o_ref, far_ref, *rest):
    out_ref, lse_ref = rest[-2:]
    rows = mixed_ref.shape[0]
    has_far = block_ref[0] >= 2
    n = HEADS_PER_STEP
    near = near_ref[...]
    far = far_ref[...]
    m_near, l_near = near[:, :n], near[:, n:]
    m_far, l_far = far[:, :n], far[:, n:]
    m = jnp.where(has_far, jnp.maximum(m_near, m_far), m_near)
    near_scale = jnp.exp(m_near - m)
    far_scale = jnp.where(has_far, jnp.exp(m_far - m), 0.0)
    total = near_scale * l_near + far_scale * l_far
    lse = m + jnp.log(total)
    inverse = 1.0 / total
    near_scale = near_scale * inverse
    far_scale = far_scale * inverse
    diagonal = lax.broadcasted_iota(jnp.int32, (rows, rows), 0) == lax.broadcasted_iota(jnp.int32, (rows, rows), 1)
    for h in range(n):
        cols = slice(h * HEAD_DIM, (h + 1) * HEAD_DIM)
        mixed = near_scale[:, h : h + 1] * mixed_ref[:, cols] + far_scale[:, h : h + 1] * o_ref[:, cols].astype(
            jnp.float32
        )
        out_ref[:, cols] = mixed.astype(out_ref.dtype)
        lse_ref[h : h + 1, :] = jnp.sum(jnp.where(diagonal, lse[:, h : h + 1], 0.0), axis=0, keepdims=True)


def merged_output(block_index, chunk, width, mixed_near, stat_near, o_far, stat_far, previous):
    rows, chunk_width = mixed_near.shape
    step_width = HEADS_PER_STEP * HEAD_DIM
    steps = chunk_width // step_width
    offset = chunk * steps
    part = pl.BlockSpec((rows, step_width), lambda g, b: (0, g))
    whole = pl.BlockSpec((rows, step_width), lambda g, b: (0, g + offset))
    lse_block = pl.BlockSpec((HEADS_PER_STEP, rows), lambda g, b: (g + offset, 0))
    operands = [block_index, mixed_near, stat_near, o_far, stat_far]
    in_specs = [part, stat_spec(rows), part, stat_spec(rows)]
    aliases = {}
    if previous is not None:
        in_specs = in_specs + [pl.BlockSpec(memory_space=pl.ANY)] * 2
        aliases = {len(operands): 0, len(operands) + 1: 1}
        operands = operands + list(previous)
    return pl.pallas_call(
        merge_kernel,
        grid_spec=pltpu.PrefetchScalarGridSpec(
            num_scalar_prefetch=1,
            grid=(steps,),
            in_specs=in_specs,
            out_specs=[whole, lse_block],
        ),
        out_shape=[
            jax.ShapeDtypeStruct((rows, width), jnp.bfloat16),
            jax.ShapeDtypeStruct((width // HEAD_DIM, rows), jnp.float32),
        ],
        input_output_aliases=aliases,
    )(*operands)


def shards(att_query, att_key, att_value):
    width = att_query.shape[1]
    chunk_width = width // CHUNKS
    index_ref = lax.axis_index("ctx").astype(jnp.int32).reshape(1)
    pieces = []
    for chunk in range(CHUNKS):
        cols = slice(chunk * chunk_width, (chunk + 1) * chunk_width)
        kv_prev = from_behind(jnp.stack([att_key[:, cols], att_value[:, cols]]), "ctx")
        q_next = from_ahead(att_query[:, cols], "ctx")
        after = (pieces[-1][1], pieces[-1][3]) if pieces else ()
        o_far, stat_far = from_behind(partial_attention(q_next, kv_prev, after), "ctx")
        mixed_near, stat_near = near_attention(index_ref, chunk, att_query, att_key, att_value, kv_prev)
        pieces.append((mixed_near, stat_near, o_far, stat_far))
    out = None
    for chunk in range(CHUNKS):
        out = merged_output(index_ref, chunk, width, *pieces[chunk], out)
    return tuple(out)


def solution(mesh):
    return jax.shard_map(
        shards,
        mesh=mesh,
        in_specs=(P(("dp", "ctx"), None), P(("dp", "ctx"), None), P(("dp", "ctx"), None)),
        out_specs=(P(("dp", "ctx"), None), P(None, ("dp", "ctx"))),
        check_vma=False,
    )
```

```python
import math

import jax
import jax.numpy as jnp
from jax import lax
from jax.experimental import pallas as pl
from jax.experimental.pallas import tpu as pltpu
from jax.sharding import PartitionSpec as P

HEAD_DIM = 128
HEADS_PER_STEP = 16
CHUNKS = 2
SCALE = 1.0 / math.sqrt(HEAD_DIM)
NT_DIMS = (((1,), (1,)), ((), ()))


def from_behind(block, axis):
    devices = range(lax.axis_size(axis))
    route = [(i - 1, i) for i in devices if i - 1 in devices]
    return lax.ppermute(block, axis, route)


def from_ahead(block, axis):
    devices = range(lax.axis_size(axis))
    route = [(i + 1, i) for i in devices if i + 1 in devices]
    return lax.ppermute(block, axis, route)


def weighted_values(weights, values):
    ones = jnp.ones((values.shape[0], HEAD_DIM), values.dtype)
    result = jnp.dot(weights, jnp.concatenate([values, ones], axis=1), preferred_element_type=jnp.float32)
    return result[:, :HEAD_DIM], result[:, HEAD_DIM : HEAD_DIM + 1]


def partial_kernel(q_ref, k_ref, v_ref, *rest):
    o_ref, stat_ref = rest[-2:]
    ones = jnp.ones((q_ref.shape[0], HEAD_DIM), jnp.bfloat16)
    for h in range(HEADS_PER_STEP):
        cols = slice(h * HEAD_DIM, (h + 1) * HEAD_DIM)
        s = lax.dot_general(q_ref[:, cols], k_ref[:, cols], NT_DIMS, preferred_element_type=jnp.float32) * SCALE
        m = jnp.max(s, axis=1, keepdims=True)
        p = jnp.exp(s - m).astype(jnp.bfloat16)
        o_ref[:, cols] = jnp.dot(p, v_ref[:, cols], preferred_element_type=jnp.float32).astype(o_ref.dtype)
        stat_ref[:, h : h + 1] = m
        total = jnp.dot(p, ones, preferred_element_type=jnp.float32)
        stat_ref[:, HEADS_PER_STEP + h : HEADS_PER_STEP + h + 1] = total[:, 0:1]


def near_kernel(block_ref, q_ref, k_ref, v_ref, kp_ref, vp_ref, mixed_ref, stat_ref):
    rows = q_ref.shape[0]
    row_id = lax.broadcasted_iota(jnp.int32, (rows, 2 * rows), 0)
    col_id = lax.broadcasted_iota(jnp.int32, (rows, 2 * rows), 1)
    first_prev = jnp.where(block_ref[0] >= 1, rows, 2 * rows)
    allowed = (col_id <= row_id) | (col_id >= first_prev)
    for h in range(HEADS_PER_STEP):
        cols = slice(h * HEAD_DIM, (h + 1) * HEAD_DIM)
        keys = jnp.concatenate([k_ref[:, cols], kp_ref[:, cols]], axis=0)
        values = jnp.concatenate([v_ref[:, cols], vp_ref[:, cols]], axis=0)
        s = lax.dot_general(q_ref[:, cols], keys, NT_DIMS, preferred_element_type=jnp.float32) * SCALE
        s = jnp.where(allowed, s, -jnp.inf)
        m = jnp.max(s, axis=1, keepdims=True)
        p = jnp.exp(s - m).astype(jnp.bfloat16)
        mixed, total = weighted_values(p, values)
        mixed_ref[:, cols] = mixed
        stat_ref[:, h : h + 1] = m
        stat_ref[:, HEADS_PER_STEP + h : HEADS_PER_STEP + h + 1] = total


def stat_spec(rows):
    return pl.BlockSpec((None, rows, 2 * HEADS_PER_STEP), lambda g, *_: (g, 0, 0))


def partial_attention(q, kv, after=()):
    rows, width = q.shape
    step_width = HEADS_PER_STEP * HEAD_DIM
    steps = width // step_width
    block = pl.BlockSpec((rows, step_width), lambda g: (0, g))
    key_block = pl.BlockSpec((None, rows, step_width), lambda g: (0, 0, g))
    value_block = pl.BlockSpec((None, rows, step_width), lambda g: (1, 0, g))
    return pl.pallas_call(
        partial_kernel,
        grid=(steps,),
        in_specs=[block, key_block, value_block] + [pl.BlockSpec(memory_space=pl.ANY)] * len(after),
        out_specs=[block, stat_spec(rows)],
        out_shape=[
            jax.ShapeDtypeStruct((rows, width), jnp.bfloat16),
            jax.ShapeDtypeStruct((steps, rows, 2 * HEADS_PER_STEP), jnp.float32),
        ],
    )(q, kv, kv, *after)


def near_attention(block_index, chunk, q, k, v, kv_prev):
    rows, width = q.shape
    step_width = HEADS_PER_STEP * HEAD_DIM
    steps = kv_prev.shape[2] // step_width
    offset = chunk * steps
    whole = pl.BlockSpec((rows, step_width), lambda g, b: (0, g + offset))
    part = pl.BlockSpec((rows, step_width), lambda g, b: (0, g))
    key_block = pl.BlockSpec((None, rows, step_width), lambda g, b: (0, 0, g))
    value_block = pl.BlockSpec((None, rows, step_width), lambda g, b: (1, 0, g))
    return pl.pallas_call(
        near_kernel,
        grid_spec=pltpu.PrefetchScalarGridSpec(
            num_scalar_prefetch=1,
            grid=(steps,),
            in_specs=[whole] * 3 + [key_block, value_block],
            out_specs=[part, stat_spec(rows)],
        ),
        out_shape=[
            jax.ShapeDtypeStruct((rows, kv_prev.shape[2]), jnp.float32),
            jax.ShapeDtypeStruct((steps, rows, 2 * HEADS_PER_STEP), jnp.float32),
        ],
    )(block_index, q, k, v, kv_prev, kv_prev)


def merge_kernel(block_ref, mixed_ref, near_ref, o_ref, far_ref, *rest):
    out_ref, lse_ref = rest[-2:]
    rows = mixed_ref.shape[0]
    has_far = block_ref[0] >= 2
    n = HEADS_PER_STEP
    near = near_ref[...]
    far = far_ref[...]
    m_near, l_near = near[:, :n], near[:, n:]
    m_far, l_far = far[:, :n], far[:, n:]
    m = jnp.where(has_far, jnp.maximum(m_near, m_far), m_near)
    near_scale = jnp.exp(m_near - m)
    far_scale = jnp.where(has_far, jnp.exp(m_far - m), 0.0)
    total = near_scale * l_near + far_scale * l_far
    lse = m + jnp.log(total)
    inverse = 1.0 / total
    near_scale = near_scale * inverse
    far_scale = far_scale * inverse
    diagonal = lax.broadcasted_iota(jnp.int32, (rows, rows), 0) == lax.broadcasted_iota(jnp.int32, (rows, rows), 1)
    for h in range(n):
        cols = slice(h * HEAD_DIM, (h + 1) * HEAD_DIM)
        mixed = near_scale[:, h : h + 1] * mixed_ref[:, cols] + far_scale[:, h : h + 1] * o_ref[:, cols].astype(
            jnp.float32
        )
        out_ref[:, cols] = mixed.astype(out_ref.dtype)
        lse_ref[h : h + 1, :] = jnp.sum(jnp.where(diagonal, lse[:, h : h + 1], 0.0), axis=0, keepdims=True)


def merged_output(block_index, chunk, width, mixed_near, stat_near, o_far, stat_far, previous):
    rows, chunk_width = mixed_near.shape
    step_width = HEADS_PER_STEP * HEAD_DIM
    steps = chunk_width // step_width
    offset = chunk * steps
    part = pl.BlockSpec((rows, step_width), lambda g, b: (0, g))
    whole = pl.BlockSpec((rows, step_width), lambda g, b: (0, g + offset))
    lse_block = pl.BlockSpec((HEADS_PER_STEP, rows), lambda g, b: (g + offset, 0))
    operands = [block_index, mixed_near, stat_near, o_far, stat_far]
    in_specs = [part, stat_spec(rows), part, stat_spec(rows)]
    aliases = {}
    if previous is not None:
        in_specs = in_specs + [pl.BlockSpec(memory_space=pl.ANY)] * 2
        aliases = {len(operands): 0, len(operands) + 1: 1}
        operands = operands + list(previous)
    return pl.pallas_call(
        merge_kernel,
        grid_spec=pltpu.PrefetchScalarGridSpec(
            num_scalar_prefetch=1,
            grid=(steps,),
            in_specs=in_specs,
            out_specs=[whole, lse_block],
        ),
        out_shape=[
            jax.ShapeDtypeStruct((rows, width), jnp.bfloat16),
            jax.ShapeDtypeStruct((width // HEAD_DIM, rows), jnp.float32),
        ],
        input_output_aliases=aliases,
    )(*operands)


def stacked_chunk(k, v, start, size):
    def kernel(k_hbm, v_hbm, o_hbm, sem):
        copies = [
            pltpu.make_async_copy(k_hbm.at[:, pl.ds(start, size)], o_hbm.at[0], sem.at[0]),
            pltpu.make_async_copy(v_hbm.at[:, pl.ds(start, size)], o_hbm.at[1], sem.at[1]),
        ]
        for copy in copies:
            copy.start()
        for copy in copies:
            copy.wait()

    return pl.pallas_call(
        kernel,
        in_specs=[pl.BlockSpec(memory_space=pl.ANY)] * 2,
        out_specs=pl.BlockSpec(memory_space=pl.ANY),
        out_shape=jax.ShapeDtypeStruct((2, k.shape[0], size), k.dtype),
        scratch_shapes=[pltpu.SemaphoreType.DMA((2,))],
    )(k, v)


def shards(att_query, att_key, att_value):
    width = att_query.shape[1]
    chunk_width = width // CHUNKS
    index_ref = lax.axis_index("ctx").astype(jnp.int32).reshape(1)
    pieces = []
    for chunk in range(CHUNKS):
        cols = slice(chunk * chunk_width, (chunk + 1) * chunk_width)
        kv_prev = from_behind(stacked_chunk(att_key, att_value, chunk * chunk_width, chunk_width), "ctx")
        q_next = from_ahead(att_query[:, cols], "ctx")
        after = (pieces[-1][1], pieces[-1][3]) if pieces else ()
        o_far, stat_far = from_behind(partial_attention(q_next, kv_prev, after), "ctx")
        mixed_near, stat_near = near_attention(index_ref, chunk, att_query, att_key, att_value, kv_prev)
        pieces.append((mixed_near, stat_near, o_far, stat_far))
    out = None
    for chunk in range(CHUNKS):
        out = merged_output(index_ref, chunk, width, *pieces[chunk], out)
    return tuple(out)


def solution(mesh):
    return jax.shard_map(
        shards,
        mesh=mesh,
        in_specs=(P(("dp", "ctx"), None), P(("dp", "ctx"), None), P(("dp", "ctx"), None)),
        out_specs=(P(("dp", "ctx"), None), P(None, ("dp", "ctx"))),
        check_vma=False,
    )
```

```python
import math

import jax
import jax.numpy as jnp
from jax import lax
from jax.experimental import pallas as pl
from jax.experimental.pallas import tpu as pltpu
from jax.sharding import PartitionSpec as P

HEAD_DIM = 128
HEADS_PER_STEP = 16
CHUNKS = 2
SCALE = 1.0 / math.sqrt(HEAD_DIM)
NT_DIMS = (((1,), (1,)), ((), ()))


def from_behind(block, axis):
    devices = range(lax.axis_size(axis))
    route = [(i - 1, i) for i in devices if i - 1 in devices]
    return lax.ppermute(block, axis, route)


def from_ahead(block, axis):
    devices = range(lax.axis_size(axis))
    route = [(i + 1, i) for i in devices if i + 1 in devices]
    return lax.ppermute(block, axis, route)


def weighted_values(weights, values):
    ones = jnp.ones((values.shape[0], HEAD_DIM), values.dtype)
    result = jnp.dot(weights, jnp.concatenate([values, ones], axis=1), preferred_element_type=jnp.float32)
    return result[:, :HEAD_DIM], result[:, HEAD_DIM : HEAD_DIM + 1]


def partial_kernel(q_ref, k_ref, v_ref, *rest):
    o_ref, stat_ref = rest[-2:]
    ones = jnp.ones((q_ref.shape[0], HEAD_DIM), jnp.bfloat16)
    for h in range(HEADS_PER_STEP):
        cols = slice(h * HEAD_DIM, (h + 1) * HEAD_DIM)
        s = lax.dot_general(q_ref[:, cols], k_ref[:, cols], NT_DIMS, preferred_element_type=jnp.float32) * SCALE
        m = jnp.max(s, axis=1, keepdims=True)
        p = jnp.exp(s - m).astype(jnp.bfloat16)
        o_ref[:, cols] = jnp.dot(p, v_ref[:, cols], preferred_element_type=jnp.float32).astype(o_ref.dtype)
        stat_ref[:, h : h + 1] = m
        total = jnp.dot(p, ones, preferred_element_type=jnp.float32)
        stat_ref[:, HEADS_PER_STEP + h : HEADS_PER_STEP + h + 1] = total[:, 0:1]


def near_kernel(block_ref, q_ref, k_ref, v_ref, kp_ref, vp_ref, mixed_ref, stat_ref):
    rows = q_ref.shape[0]
    row_id = lax.broadcasted_iota(jnp.int32, (rows, 2 * rows), 0)
    col_id = lax.broadcasted_iota(jnp.int32, (rows, 2 * rows), 1)
    first_prev = jnp.where(block_ref[0] >= 1, rows, 2 * rows)
    allowed = (col_id <= row_id) | (col_id >= first_prev)
    for h in range(HEADS_PER_STEP):
        cols = slice(h * HEAD_DIM, (h + 1) * HEAD_DIM)
        keys = jnp.concatenate([k_ref[:, cols], kp_ref[:, cols]], axis=0)
        values = jnp.concatenate([v_ref[:, cols], vp_ref[:, cols]], axis=0)
        s = lax.dot_general(q_ref[:, cols], keys, NT_DIMS, preferred_element_type=jnp.float32) * SCALE
        s = jnp.where(allowed, s, -jnp.inf)
        m = jnp.max(s, axis=1, keepdims=True)
        p = jnp.exp(s - m).astype(jnp.bfloat16)
        mixed, total = weighted_values(p, values)
        mixed_ref[:, cols] = mixed
        stat_ref[:, h : h + 1] = m
        stat_ref[:, HEADS_PER_STEP + h : HEADS_PER_STEP + h + 1] = total


def stat_spec(rows):
    return pl.BlockSpec((None, rows, 2 * HEADS_PER_STEP), lambda g, *_: (g, 0, 0))


def partial_attention(q, kv, after=()):
    rows, width = q.shape
    step_width = HEADS_PER_STEP * HEAD_DIM
    steps = width // step_width
    block = pl.BlockSpec((rows, step_width), lambda g: (0, g))
    key_block = pl.BlockSpec((None, rows, step_width), lambda g: (0, 0, g))
    value_block = pl.BlockSpec((None, rows, step_width), lambda g: (1, 0, g))
    return pl.pallas_call(
        partial_kernel,
        grid=(steps,),
        in_specs=[block, key_block, value_block] + [pl.BlockSpec(memory_space=pl.ANY)] * len(after),
        out_specs=[block, stat_spec(rows)],
        out_shape=[
            jax.ShapeDtypeStruct((rows, width), jnp.bfloat16),
            jax.ShapeDtypeStruct((steps, rows, 2 * HEADS_PER_STEP), jnp.float32),
        ],
    )(q, kv, kv, *after)


def near_attention(block_index, chunk, q, k, v, kv_prev):
    rows, width = q.shape
    step_width = HEADS_PER_STEP * HEAD_DIM
    steps = kv_prev.shape[2] // step_width
    offset = chunk * steps
    whole = pl.BlockSpec((rows, step_width), lambda g, b: (0, g + offset))
    part = pl.BlockSpec((rows, step_width), lambda g, b: (0, g))
    key_block = pl.BlockSpec((None, rows, step_width), lambda g, b: (0, 0, g))
    value_block = pl.BlockSpec((None, rows, step_width), lambda g, b: (1, 0, g))
    return pl.pallas_call(
        near_kernel,
        grid_spec=pltpu.PrefetchScalarGridSpec(
            num_scalar_prefetch=1,
            grid=(steps,),
            in_specs=[whole] * 3 + [key_block, value_block],
            out_specs=[part, stat_spec(rows)],
        ),
        out_shape=[
            jax.ShapeDtypeStruct((rows, kv_prev.shape[2]), jnp.float32),
            jax.ShapeDtypeStruct((steps, rows, 2 * HEADS_PER_STEP), jnp.float32),
        ],
    )(block_index, q, k, v, kv_prev, kv_prev)


def merge_kernel(block_ref, mixed_ref, near_ref, o_ref, far_ref, *rest):
    out_ref, lse_ref = rest[-2:]
    rows = mixed_ref.shape[0]
    has_far = block_ref[0] >= 2
    n = HEADS_PER_STEP
    near = near_ref[...]
    far = far_ref[...]
    m_near, l_near = near[:, :n], near[:, n:]
    m_far, l_far = far[:, :n], far[:, n:]
    m = jnp.where(has_far, jnp.maximum(m_near, m_far), m_near)
    near_scale = jnp.exp(m_near - m)
    far_scale = jnp.where(has_far, jnp.exp(m_far - m), 0.0)
    total = near_scale * l_near + far_scale * l_far
    lse = m + jnp.log(total)
    inverse = 1.0 / total
    near_scale = near_scale * inverse
    far_scale = far_scale * inverse
    diagonal = lax.broadcasted_iota(jnp.int32, (rows, rows), 0) == lax.broadcasted_iota(jnp.int32, (rows, rows), 1)
    for h in range(n):
        cols = slice(h * HEAD_DIM, (h + 1) * HEAD_DIM)
        mixed = near_scale[:, h : h + 1] * mixed_ref[:, cols] + far_scale[:, h : h + 1] * o_ref[:, cols].astype(
            jnp.float32
        )
        out_ref[:, cols] = mixed.astype(out_ref.dtype)
        lse_ref[h : h + 1, :] = jnp.sum(jnp.where(diagonal, lse[:, h : h + 1], 0.0), axis=0, keepdims=True)


def merged_output(block_index, chunk, width, mixed_near, stat_near, o_far, stat_far, previous):
    rows, chunk_width = mixed_near.shape
    step_width = HEADS_PER_STEP * HEAD_DIM
    steps = chunk_width // step_width
    offset = chunk * steps
    part = pl.BlockSpec((rows, step_width), lambda g, b: (0, g))
    whole = pl.BlockSpec((rows, step_width), lambda g, b: (0, g + offset))
    lse_block = pl.BlockSpec((HEADS_PER_STEP, rows), lambda g, b: (g + offset, 0))
    operands = [block_index, mixed_near, stat_near, o_far, stat_far]
    in_specs = [part, stat_spec(rows), part, stat_spec(rows)]
    aliases = {}
    if previous is not None:
        in_specs = in_specs + [pl.BlockSpec(memory_space=pl.ANY)] * 2
        aliases = {len(operands): 0, len(operands) + 1: 1}
        operands = operands + list(previous)
    return pl.pallas_call(
        merge_kernel,
        grid_spec=pltpu.PrefetchScalarGridSpec(
            num_scalar_prefetch=1,
            grid=(steps,),
            in_specs=in_specs,
            out_specs=[whole, lse_block],
        ),
        out_shape=[
            jax.ShapeDtypeStruct((rows, width), jnp.bfloat16),
            jax.ShapeDtypeStruct((width // HEAD_DIM, rows), jnp.float32),
        ],
        input_output_aliases=aliases,
    )(*operands)


def stacked_chunk(k, v, chunk, size):
    def kernel(k_ref, v_ref, o_ref):
        o_ref[0] = k_ref[...]
        o_ref[1] = v_ref[...]

    rows = k.shape[0]
    block = pl.BlockSpec((rows, size), lambda i: (0, chunk))
    return pl.pallas_call(
        kernel,
        grid=(1,),
        in_specs=[block, block],
        out_specs=pl.BlockSpec((2, rows, size), lambda i: (0, 0, 0)),
        out_shape=jax.ShapeDtypeStruct((2, rows, size), k.dtype),
    )(k, v)


def shards(att_query, att_key, att_value):
    width = att_query.shape[1]
    chunk_width = width // CHUNKS
    index_ref = lax.axis_index("ctx").astype(jnp.int32).reshape(1)
    pieces = []
    for chunk in range(CHUNKS):
        cols = slice(chunk * chunk_width, (chunk + 1) * chunk_width)
        kv_prev = from_behind(stacked_chunk(att_key, att_value, chunk, chunk_width), "ctx")
        q_next = from_ahead(att_query[:, cols], "ctx")
        after = (pieces[-1][1], pieces[-1][3]) if pieces else ()
        o_far, stat_far = from_behind(partial_attention(q_next, kv_prev, after), "ctx")
        mixed_near, stat_near = near_attention(index_ref, chunk, att_query, att_key, att_value, kv_prev)
        pieces.append((mixed_near, stat_near, o_far, stat_far))
    out = None
    for chunk in range(CHUNKS):
        out = merged_output(index_ref, chunk, width, *pieces[chunk], out)
    return tuple(out)


def solution(mesh):
    return jax.shard_map(
        shards,
        mesh=mesh,
        in_specs=(P(("dp", "ctx"), None), P(("dp", "ctx"), None), P(("dp", "ctx"), None)),
        out_specs=(P(("dp", "ctx"), None), P(None, ("dp", "ctx"))),
        check_vma=False,
    )
```

```python
import math

import jax
import jax.numpy as jnp
from jax import lax
from jax.experimental import pallas as pl
from jax.experimental.pallas import tpu as pltpu
from jax.sharding import PartitionSpec as P

HEAD_DIM = 128
HEADS_PER_STEP = 16
CHUNKS = 2
SCALE = 1.0 / math.sqrt(HEAD_DIM)
NT_DIMS = (((1,), (1,)), ((), ()))


def from_behind(block, axis):
    devices = range(lax.axis_size(axis))
    route = [(i - 1, i) for i in devices if i - 1 in devices]
    return lax.ppermute(block, axis, route)


def from_ahead(block, axis):
    devices = range(lax.axis_size(axis))
    route = [(i + 1, i) for i in devices if i + 1 in devices]
    return lax.ppermute(block, axis, route)


def weighted_values(weights, values):
    ones = jnp.ones((values.shape[0], HEAD_DIM), values.dtype)
    result = jnp.dot(weights, jnp.concatenate([values, ones], axis=1), preferred_element_type=jnp.float32)
    return result[:, :HEAD_DIM], result[:, HEAD_DIM : HEAD_DIM + 1]


def partial_kernel(q_ref, k_ref, v_ref, *rest):
    o_ref, stat_ref = rest[-2:]
    ones = jnp.ones((q_ref.shape[0], HEAD_DIM), jnp.bfloat16)
    for h in range(HEADS_PER_STEP):
        cols = slice(h * HEAD_DIM, (h + 1) * HEAD_DIM)
        s = lax.dot_general(q_ref[:, cols], k_ref[:, cols], NT_DIMS, preferred_element_type=jnp.float32) * SCALE
        m = jnp.max(s, axis=1, keepdims=True)
        p = jnp.exp(s - m).astype(jnp.bfloat16)
        o_ref[:, cols] = jnp.dot(p, v_ref[:, cols], preferred_element_type=jnp.float32).astype(o_ref.dtype)
        stat_ref[:, h : h + 1] = m
        total = jnp.dot(p, ones, preferred_element_type=jnp.float32)
        stat_ref[:, HEADS_PER_STEP + h : HEADS_PER_STEP + h + 1] = total[:, 0:1]


def near_kernel(block_ref, q_ref, k_ref, v_ref, kp_ref, vp_ref, mixed_ref, stat_ref):
    rows = q_ref.shape[0]
    row_id = lax.broadcasted_iota(jnp.int32, (rows, 2 * rows), 0)
    col_id = lax.broadcasted_iota(jnp.int32, (rows, 2 * rows), 1)
    first_prev = jnp.where(block_ref[0] >= 1, rows, 2 * rows)
    allowed = (col_id <= row_id) | (col_id >= first_prev)
    for h in range(HEADS_PER_STEP):
        cols = slice(h * HEAD_DIM, (h + 1) * HEAD_DIM)
        keys = jnp.concatenate([k_ref[:, cols], kp_ref[:, cols]], axis=0)
        values = jnp.concatenate([v_ref[:, cols], vp_ref[:, cols]], axis=0)
        s = lax.dot_general(q_ref[:, cols], keys, NT_DIMS, preferred_element_type=jnp.float32) * SCALE
        s = jnp.where(allowed, s, -jnp.inf)
        m = jnp.max(s, axis=1, keepdims=True)
        p = jnp.exp(s - m).astype(jnp.bfloat16)
        mixed, total = weighted_values(p, values)
        mixed_ref[:, cols] = mixed
        stat_ref[:, h : h + 1] = m
        stat_ref[:, HEADS_PER_STEP + h : HEADS_PER_STEP + h + 1] = total


def stat_spec(rows):
    return pl.BlockSpec((None, rows, 2 * HEADS_PER_STEP), lambda g, *_: (g, 0, 0))


def partial_attention(q, kv, after=()):
    rows, width = q.shape
    step_width = HEADS_PER_STEP * HEAD_DIM
    steps = width // step_width
    block = pl.BlockSpec((rows, step_width), lambda g: (0, g))
    key_block = pl.BlockSpec((None, rows, step_width), lambda g: (0, 0, g))
    value_block = pl.BlockSpec((None, rows, step_width), lambda g: (1, 0, g))
    return pl.pallas_call(
        partial_kernel,
        grid=(steps,),
        in_specs=[block, key_block, value_block] + [pl.BlockSpec(memory_space=pl.ANY)] * len(after),
        out_specs=[block, stat_spec(rows)],
        out_shape=[
            jax.ShapeDtypeStruct((rows, width), jnp.bfloat16),
            jax.ShapeDtypeStruct((steps, rows, 2 * HEADS_PER_STEP), jnp.float32),
        ],
    )(q, kv, kv, *after)


def near_attention(block_index, chunk, q, k, v, kv_prev):
    rows, width = q.shape
    step_width = HEADS_PER_STEP * HEAD_DIM
    steps = kv_prev.shape[2] // step_width
    offset = chunk * steps
    whole = pl.BlockSpec((rows, step_width), lambda g, b: (0, g + offset))
    part = pl.BlockSpec((rows, step_width), lambda g, b: (0, g))
    key_block = pl.BlockSpec((None, rows, step_width), lambda g, b: (0, 0, g))
    value_block = pl.BlockSpec((None, rows, step_width), lambda g, b: (1, 0, g))
    return pl.pallas_call(
        near_kernel,
        grid_spec=pltpu.PrefetchScalarGridSpec(
            num_scalar_prefetch=1,
            grid=(steps,),
            in_specs=[whole] * 3 + [key_block, value_block],
            out_specs=[part, stat_spec(rows)],
        ),
        out_shape=[
            jax.ShapeDtypeStruct((rows, kv_prev.shape[2]), jnp.float32),
            jax.ShapeDtypeStruct((steps, rows, 2 * HEADS_PER_STEP), jnp.float32),
        ],
    )(block_index, q, k, v, kv_prev, kv_prev)


def merge_kernel(block_ref, mixed_ref, near_ref, o_ref, far_ref, *rest):
    out_ref, lse_ref = rest[-2:]
    rows = mixed_ref.shape[0]
    has_far = block_ref[0] >= 2
    n = HEADS_PER_STEP
    near = near_ref[...]
    far = far_ref[...]
    m_near, l_near = near[:, :n], near[:, n:]
    m_far, l_far = far[:, :n], far[:, n:]
    m = jnp.where(has_far, jnp.maximum(m_near, m_far), m_near)
    near_scale = jnp.exp(m_near - m)
    far_scale = jnp.where(has_far, jnp.exp(m_far - m), 0.0)
    total = near_scale * l_near + far_scale * l_far
    lse = m + jnp.log(total)
    inverse = 1.0 / total
    near_scale = near_scale * inverse
    far_scale = far_scale * inverse
    identity = (lax.broadcasted_iota(jnp.int32, (n, n), 0) == lax.broadcasted_iota(jnp.int32, (n, n), 1)).astype(
        jnp.float32
    )
    for h in range(n):
        cols = slice(h * HEAD_DIM, (h + 1) * HEAD_DIM)
        mixed = near_scale[:, h : h + 1] * mixed_ref[:, cols] + far_scale[:, h : h + 1] * o_ref[:, cols].astype(
            jnp.float32
        )
        out_ref[:, cols] = mixed.astype(out_ref.dtype)
    lse_ref[...] = lax.dot_general(
        identity, lse, NT_DIMS, precision=lax.Precision.HIGHEST, preferred_element_type=jnp.float32
    )


def merged_output(block_index, chunk, width, mixed_near, stat_near, o_far, stat_far, previous):
    rows, chunk_width = mixed_near.shape
    step_width = HEADS_PER_STEP * HEAD_DIM
    steps = chunk_width // step_width
    offset = chunk * steps
    part = pl.BlockSpec((rows, step_width), lambda g, b: (0, g))
    whole = pl.BlockSpec((rows, step_width), lambda g, b: (0, g + offset))
    lse_block = pl.BlockSpec((HEADS_PER_STEP, rows), lambda g, b: (g + offset, 0))
    operands = [block_index, mixed_near, stat_near, o_far, stat_far]
    in_specs = [part, stat_spec(rows), part, stat_spec(rows)]
    aliases = {}
    if previous is not None:
        in_specs = in_specs + [pl.BlockSpec(memory_space=pl.ANY)] * 2
        aliases = {len(operands): 0, len(operands) + 1: 1}
        operands = operands + list(previous)
    return pl.pallas_call(
        merge_kernel,
        grid_spec=pltpu.PrefetchScalarGridSpec(
            num_scalar_prefetch=1,
            grid=(steps,),
            in_specs=in_specs,
            out_specs=[whole, lse_block],
        ),
        out_shape=[
            jax.ShapeDtypeStruct((rows, width), jnp.bfloat16),
            jax.ShapeDtypeStruct((width // HEAD_DIM, rows), jnp.float32),
        ],
        input_output_aliases=aliases,
    )(*operands)


def shards(att_query, att_key, att_value):
    width = att_query.shape[1]
    chunk_width = width // CHUNKS
    index_ref = lax.axis_index("ctx").astype(jnp.int32).reshape(1)
    pieces = []
    for chunk in range(CHUNKS):
        cols = slice(chunk * chunk_width, (chunk + 1) * chunk_width)
        kv_prev = from_behind(jnp.stack([att_key[:, cols], att_value[:, cols]]), "ctx")
        q_next = from_ahead(att_query[:, cols], "ctx")
        after = (pieces[-1][1], pieces[-1][3]) if pieces else ()
        o_far, stat_far = from_behind(partial_attention(q_next, kv_prev, after), "ctx")
        mixed_near, stat_near = near_attention(index_ref, chunk, att_query, att_key, att_value, kv_prev)
        pieces.append((mixed_near, stat_near, o_far, stat_far))
    out = None
    for chunk in range(CHUNKS):
        out = merged_output(index_ref, chunk, width, *pieces[chunk], out)
    return tuple(out)


def solution(mesh):
    return jax.shard_map(
        shards,
        mesh=mesh,
        in_specs=(P(("dp", "ctx"), None), P(("dp", "ctx"), None), P(("dp", "ctx"), None)),
        out_specs=(P(("dp", "ctx"), None), P(None, ("dp", "ctx"))),
        check_vma=False,
    )
```
